512 devices in a mesh: gx: 8 (over z_lo, x), gy: 16 (over y, core), gz: 4 (over z_hi).
Axes of the slice: x: 4, y: 8, z: 8 (z_hi: 4, z_lo: 2; z = z_hi * 2 + z_lo), core: 2. Of those that a mesh axis runs over, the one named last changes fastest.
Arguments:
- positions: float32 [3, 262144], P(None, ('gx', 'gy', 'gz')), may hold values from 0 to 1
- velocities: float32 [3, 262144], P(None, ('gx', 'gy', 'gz')), may hold values from -5 to 5
- neighbour_index: int32 [24, 262144], P(None, ('gx', 'gy', 'gz')), may hold values from 0 to 3967, as said below
- neighbour_count: int32 [262144], P(('gx', 'gy', 'gz')), may hold values from 0 to 24, as said below
- ghost_list: int32 [65536], P(('gx', 'gy', 'gz')), may hold values from 0 to 511, as said below
- brick_count: int32 [512], P(('gx', 'gy', 'gz')), may hold values from 128 to 512, as said below
- atom_cell: int32 [262144], P(('gx', 'gy', 'gz')), may hold values from 0 to 127
- radial_weight: float32 [16, 8], replicated, may hold values from -2 to 2
- linear_weight: float32 [16], replicated, may hold values from -4 to 4
- pair_coupling: float32 [4, 16, 16], replicated, may hold values from -0.375 to 0.375
- electron_temp: float32 [16, 64, 64], P('gz', 'gy', 'gx'), may hold values from 1 to 2
- conductivity: float32 [16, 64, 64], P('gz', 'gy', 'gx'), may hold values from 0.3 to 1
- heating: float32 [16, 64, 64], P('gz', 'gy', 'gx'), may hold values from 0.05 to 1
Outputs:
- forces: float32 [3, 262144], P(None, ('gx', 'gy', 'gz'))
- new_velocity: float32 [3, 262144], P(None, ('gx', 'gy', 'gz'))
- new_electron_temp: float32 [16, 64, 64], P('gz', 'gy', 'gx')
- totals: float32 [10], replicated
The draws below stay inside these ranges and needn't reach their ends.
Inputs may be any that keep to these rules, and one draw needn't show every extreme that they name: `brick_count`: bricks with b % 4 == 3 are full. `ghost_list`: entries of brick b name live atoms of brick b. `neighbour_count`: zero for atoms that are not live, at least 12 for live ones. `neighbour_index`: A used entry below 512 names a live atom of the same brick; otherwise it is 512 + s * 128 + g with slot s != 13, and never a slot whose depth offset crosses the film's surface (o2 = -1 in bricks with bz = 0, o2 = 1 in bricks with bz = 3).
All inputs are finite; a program needn't handle non-finite values.
Results may differ from the reference program's by a relative error of at most 0.0003.
Values sent between devices are 32-bit elements; how exact they have to be, the bound alone decides.
No kernel may reach another device: no remote copies, remote signals or barrier semaphores. Data moves between devices by JAX's collectives and lax.ppermute only.
A program may use at most 64 MiB of HBM per device.

```python
import math
import jax
import jax.numpy as jnp
from jax import lax

ATOMS_DEV = 512
GHOSTS_DEV = 128
NEIGH = 24
NR = 16
NC = 8
NY = 16
SUBSTEPS = 4
CXD = 8
CYD = 4
CZD = 4
BRICKS = 512
BRICKS_Z = 4
ATOMS = 262144
CELLS_DEV = 128
NCX = 64
NCY = 64
NCZ = 16
N_GX = 8
N_GY = 16
N_GZ = 4


def live_counts(key):
    depth_layer = jnp.arange(BRICKS) % BRICKS_Z
    floors = ATOMS_DEV // 4 + ATOMS_DEV // 2 * depth_layer // (BRICKS_Z - 1)
    drawn = jax.random.randint(jax.random.fold_in(key, 7), (BRICKS,), floors, ATOMS_DEV + 1)
    return jnp.where(depth_layer == BRICKS_Z - 1, ATOMS_DEV, drawn).astype(jnp.int32)


def draw_brick_count(key, part):
    return live_counts(key)


def draw_ghost_list(key, part):
    counts_live = live_counts(key)
    raw_bits = jax.random.randint(jax.random.fold_in(key, 11), (BRICKS, GHOSTS_DEV), 0, 1 << 30)
    picked = raw_bits % counts_live[:, None]
    picked = picked.at[:, 0].set(0)
    picked = picked.at[:, -1].set(counts_live - 1)
    return picked.reshape(-1).astype(jnp.int32)


def draw_neighbour_count(key, part):
    counts_live = live_counts(key)
    drawn = jax.random.randint(jax.random.fold_in(key, 13), (BRICKS, ATOMS_DEV), NEIGH // 2, NEIGH + 1)
    drawn = drawn.at[:, 0].set(NEIGH)
    living = jnp.arange(ATOMS_DEV)[None, :] < counts_live[:, None]
    return jnp.where(living, drawn, 0).reshape(-1).astype(jnp.int32)


def draw_neighbour_index(key, part):
    counts_live = live_counts(key)
    tile_shape = (BRICKS, NEIGH, ATOMS_DEV)
    key_list = jax.random.split(jax.random.fold_in(key, 17), 6)
    inside = jax.random.randint(key_list[0], tile_shape, 0, 1 << 30) % counts_live[:, None, None]
    depth_layer = (jnp.arange(BRICKS) % BRICKS_Z)[:, None, None]
    lowest = jnp.where(depth_layer == 0, 1, 0)
    highest = jnp.where(depth_layer == BRICKS_Z - 1, 1, 2)
    step_x = jax.random.randint(key_list[1], tile_shape, 0, 3)
    step_y = jax.random.randint(key_list[2], tile_shape, 0, 3)
    step_z = lowest + jax.random.randint(key_list[3], tile_shape, 0, 1 << 30) % (highest - lowest + 1)
    centre = (step_x == 1) & (step_y == 1) & (step_z == 1)
    step_x = jnp.where(centre, 0, step_x)
    member = jax.random.randint(key_list[4], tile_shape, 0, GHOSTS_DEV)
    remote = ATOMS_DEV + (9 * step_x + 3 * step_y + step_z) * GHOSTS_DEV + member
    choose = jax.random.randint(key_list[5], tile_shape, 0, 2)
    chosen = jnp.where(choose == 0, inside, remote)
    chosen = chosen.at[:, 1, 0].set(0)
    corner_value = jnp.where(depth_layer[:, 0, 0] == BRICKS_Z - 1, chosen[:, 0, 0], ATOMS_DEV + 27 * GHOSTS_DEV - 1)
    chosen = chosen.at[:, 0, 0].set(corner_value)
    return jnp.transpose(chosen, (1, 0, 2)).reshape(NEIGH, ATOMS).astype(jnp.int32)


def place_ends(entries, key, least, top_value):
    extent = entries.shape
    place = [jax.random.randint(jax.random.fold_in(key, axis), (), 0, extent[axis]) for axis in range(len(extent))]
    entries = entries.at[tuple(place)].set(least)
    longest = extent.index(max(extent))
    place[longest] = (place[longest] + 1) % extent[longest]
    return entries.at[tuple(place)].set(top_value)


def level_of(rng, shape, cuts, smallest, top_value):
    level = 1.0
    for dim, blocks in cuts:
        heights = jax.random.uniform(jax.random.fold_in(jax.random.fold_in(rng, 6), dim), (blocks,), jnp.float32, smallest / len(cuts), top_value / len(cuts))
        level = level * jnp.repeat(jnp.exp(heights), shape[dim] // blocks).reshape((-1,) + (1,) * (len(shape) - 1 - dim))
    return level


def scatter_about(stream_key, dims, scale, bound, shards=(), held_as=jnp.bfloat16):
    entries = scale * jax.random.normal(stream_key, dims, jnp.float32)
    if shards:
        entries = entries * level_of(stream_key, dims, shards, -0.22, 0.18)
    return jnp.clip(entries, -bound, bound).astype(held_as)


def setup_inputs(seed: int = 0) -> dict:
    seeds = jax.random.split(jax.random.key(seed), 14)
    positions = jnp.clip(1.0 * jax.random.uniform(seeds[0], (3, ATOMS), jnp.float32) ** level_of(seeds[0], (3, ATOMS), ((1, 512),), -0.2, 0.2), 0.0, 1.0)
    velocities = scatter_about(seeds[1], (3, ATOMS), 1.0, 5.0, ((1, 512),), jnp.float32)
    neighbour_index = draw_neighbour_index(jax.random.fold_in(seeds[13], 71), 0)
    neighbour_count = draw_neighbour_count(jax.random.fold_in(seeds[13], 71), 0)
    ghost_list = draw_ghost_list(jax.random.fold_in(seeds[13], 71), 0)
    brick_count = draw_brick_count(jax.random.fold_in(seeds[13], 71), 0)
    atom_cell = place_ends(jax.random.randint(seeds[6], (ATOMS,), 0, CELLS_DEV), jax.random.fold_in(seeds[6], 1), 0, CELLS_DEV - 1).astype(jnp.int32)
    radial_weight = scatter_about(seeds[7], (NR, NC), NC ** -0.5, 2.0, (), jnp.float32)
    linear_weight = scatter_about(seeds[8], (NR,), 1.0, 4.0, (), jnp.float32)
    pair_coupling = scatter_about(seeds[9], (4, NR, NR), (NR * NY) ** -0.5, 0.375, (), jnp.float32)
    electron_temp = jnp.clip(1.0 + 1.0 * jax.random.uniform(seeds[10], (NCZ, NCY, NCX), jnp.float32) ** level_of(seeds[10], (NCZ, NCY, NCX), ((0, 4), (1, 16), (2, 8)), -0.2, 0.2), 1.0, 2.0)
    conductivity = jnp.clip(jnp.exp(math.log(1.0) - 1.2039728 * jax.random.uniform(seeds[11], (NCZ, NCY, NCX), jnp.float32) ** level_of(seeds[11], (NCZ, NCY, NCX), ((0, 4), (1, 16), (2, 8)), -0.2, 0.2)), 0.3, 1.0)
    heating = jnp.clip(jnp.exp(math.log(1.0) - 2.9957323 * jax.random.uniform(seeds[12], (NCZ, NCY, NCX), jnp.float32) ** level_of(seeds[12], (NCZ, NCY, NCX), ((0, 4), (1, 16), (2, 8)), -0.2, 0.2)), 0.05, 1.0)
    return dict(positions=positions, velocities=velocities, neighbour_index=neighbour_index, neighbour_count=neighbour_count, ghost_list=ghost_list, brick_count=brick_count, atom_cell=atom_cell, radial_weight=radial_weight, linear_weight=linear_weight, pair_coupling=pair_coupling, electron_temp=electron_temp, conductivity=conductivity, heating=heating)


HEAT_STEP = 0.15
COUPLE = 0.5
RELAX = 0.2
KICK = 0.05
SPREAD = 2.0
ROOT_THREE = 1.7320508

def harmonics(vector):
    coord_x, coord_y, coord_z = (vector[0], vector[1], vector[2])
    radius_sq = coord_x * coord_x + coord_y * coord_y + coord_z * coord_z
    terms = [jnp.ones_like(coord_x), coord_x, coord_y, coord_z, ROOT_THREE * coord_x * coord_y, ROOT_THREE * coord_y * coord_z, 0.5 * (3.0 * coord_z * coord_z - radius_sq), ROOT_THREE * coord_x * coord_z, 0.5 * ROOT_THREE * (coord_x * coord_x - coord_y * coord_y), 0.79 * coord_y * (3.0 * coord_x * coord_x - coord_y * coord_y), 3.87 * coord_x * coord_y * coord_z, 0.61 * coord_y * (4.0 * coord_z * coord_z - coord_x * coord_x - coord_y * coord_y), 0.5 * coord_z * (2.0 * coord_z * coord_z - 3.0 * coord_x * coord_x - 3.0 * coord_y * coord_y), 0.61 * coord_x * (4.0 * coord_z * coord_z - coord_x * coord_x - coord_y * coord_y), 1.94 * coord_z * (coord_x * coord_x - coord_y * coord_y), 0.79 * coord_x * (coord_x * coord_x - 3.0 * coord_y * coord_y)]
    return jnp.stack(terms)

def radial(vector, orders):
    radius_sq = lax.optimization_barrier(jnp.sum(vector * vector, axis=0))
    decay = jnp.exp(-radius_sq / SPREAD)
    argument = 2.0 * decay - 1.0
    polys = [jnp.ones_like(argument), argument]
    for order_id in range(2, orders):
        polys.append(2.0 * argument * polys[-1] - polys[-2])
    return decay * jnp.stack(polys[:orders])

def pair_energy(vector, weights):
    basis = radial(vector, weights.shape[0])
    mixed = lax.optimization_barrier(jnp.sum(weights * basis[:, None], axis=0))
    return lax.optimization_barrier(jnp.sum(mixed * harmonics(vector), axis=0))

def atom_basis(separation, pair_mask, radial_weight):
    basis = radial(separation, radial_weight.shape[1])
    shaped = jnp.einsum('nc,cka->nka', radial_weight, basis, precision=lax.Precision.HIGHEST) * pair_mask
    return jnp.einsum('nka,mka->nma', shaped, harmonics(separation), precision=lax.Precision.HIGHEST)

def adjoints(basis_sum, linear_weight, pair_coupling):
    per_harmonic = jnp.concatenate([jnp.repeat(pair_coupling[degree_id:degree_id + 1], copies, axis=0) for degree_id, copies in enumerate((1, 3, 5, 7))], axis=0)
    forward = jnp.einsum('mnp,pma->nma', per_harmonic, basis_sum, precision=lax.Precision.HIGHEST)
    backward = jnp.einsum('mpn,pma->nma', per_harmonic, basis_sum, precision=lax.Precision.HIGHEST)
    energy = jnp.dot(linear_weight, basis_sum[:, 0, :], precision=lax.Precision.HIGHEST) + lax.optimization_barrier(jnp.sum(basis_sum * forward, axis=(0, 1)))
    adjoint = (forward + backward).at[:, 0, :].add(linear_weight[:, None])
    return (energy, adjoint)

def contract(radial_weight, adjoint):
    return jnp.einsum('nc,nma->cma', radial_weight, adjoint, precision=lax.Precision.HIGHEST)

def pair_forces(separation, pair_mask, own_weights, other_weights):
    own_grad = jax.grad(lambda vector: jnp.sum(pair_energy(vector, own_weights)))(separation)
    other_grad = jax.grad(lambda vector: jnp.sum(pair_energy(vector, other_weights)))(-separation)
    pieces = (own_grad - other_grad) * pair_mask
    return (lax.optimization_barrier(jnp.sum(pieces, axis=1)), jnp.einsum('aki,bki->ab', separation, pieces, precision=lax.Precision.HIGHEST))

def diffuse(electron, conductivity, heating, lattice, occupancy):
    layers = electron.shape[0]
    depth_ids = jnp.arange(layers)
    upper_open = (depth_ids != layers - 1).astype(jnp.float32)[:, None, None]
    lower_open = (depth_ids != 0).astype(jnp.float32)[:, None, None]
    for substep_id in range(SUBSTEPS):
        kappa = conductivity * electron

        def face(axis_id, offset):
            beside_temp = jnp.roll(electron, offset, axis_id)
            beside_kappa = jnp.roll(kappa, offset, axis_id)
            return 0.5 * (kappa + beside_kappa) * (beside_temp - electron)
        divergence = face(2, -1) + face(2, 1) + face(1, -1) + face(1, 1) + face(0, -1) * upper_open + face(0, 1) * lower_open
        electron = electron + HEAT_STEP / electron * (divergence + heating - COUPLE * occupancy * (electron - lattice))
    return electron

def to_grid(per_brick):
    blocks = per_brick.reshape(N_GX, N_GY, N_GZ, CZD, CYD, CXD)
    return jnp.transpose(blocks, (2, 3, 1, 4, 0, 5)).reshape(NCZ, NCY, NCX)

def from_grid(grid_field):
    blocks = grid_field.reshape(N_GZ, CZD, N_GY, CYD, N_GX, CXD)
    return jnp.transpose(blocks, (4, 2, 0, 1, 3, 5)).reshape(N_GX * N_GY * N_GZ, CZD * CYD * CXD)

def reference(positions, velocities, neighbour_index, neighbour_count, ghost_list, brick_count, atom_cell, radial_weight, linear_weight, pair_coupling, electron_temp, conductivity, heating):
    brick_total = N_GX * N_GY * N_GZ
    cell_total = CZD * CYD * CXD
    pos_bricks = jnp.transpose(positions.reshape(3, brick_total, ATOMS_DEV), (1, 0, 2))
    index_bricks = jnp.transpose(neighbour_index.reshape(NEIGH, brick_total, ATOMS_DEV), (1, 0, 2))
    count_bricks = neighbour_count.reshape(brick_total, ATOMS_DEV)
    ghost_bricks = ghost_list.reshape(brick_total, GHOSTS_DEV)
    ghost_pos = jnp.take_along_axis(pos_bricks, ghost_bricks[:, None, :], axis=2)
    brick_ids = jnp.arange(brick_total)
    along_x = brick_ids // (N_GY * N_GZ)
    along_y = brick_ids // N_GZ % N_GY
    along_z = brick_ids % N_GZ
    slot_ids = jnp.arange(27)
    shift_x = slot_ids // 9 - 1
    shift_y = slot_ids // 3 % 3 - 1
    shift_z = slot_ids % 3 - 1
    beside_bricks = ((along_x[:, None] + shift_x[None, :]) % N_GX * N_GY + (along_y[:, None] + shift_y[None, :]) % N_GY) * N_GZ + (along_z[:, None] + shift_z[None, :]) % N_GZ
    offsets = jnp.stack([shift_x, shift_y, shift_z], axis=1).astype(jnp.float32)
    neigh_ids = jnp.arange(NEIGH)

    def geometry(brick):
        ghosts_here = ghost_pos[beside_bricks[brick]] + offsets[:, :, None]
        table = jnp.concatenate([pos_bricks[brick], jnp.transpose(ghosts_here, (1, 0, 2)).reshape(3, 27 * GHOSTS_DEV)], axis=1)
        separation = table[:, index_bricks[brick]] - pos_bricks[brick][:, None, :]
        pair_mask = (neigh_ids[:, None] < count_bricks[brick][None, :]).astype(jnp.float32)
        return (separation, pair_mask)

    def first_pass(brick):
        separation, pair_mask = geometry(brick)
        basis_sum = atom_basis(separation, pair_mask, radial_weight)
        energy, adjoint = adjoints(basis_sum, linear_weight, pair_coupling)
        return (energy, contract(radial_weight, adjoint).reshape(NC * 16, ATOMS_DEV))
    energies, reduced_bricks = lax.map(first_pass, brick_ids)
    reduced_ghosts = jnp.take_along_axis(reduced_bricks, ghost_bricks[:, None, :], axis=2)

    def second_pass(brick):
        separation, pair_mask = geometry(brick)
        remote = reduced_ghosts[beside_bricks[brick]]
        table = jnp.concatenate([reduced_bricks[brick], jnp.transpose(remote, (1, 0, 2)).reshape(NC * 16, 27 * GHOSTS_DEV)], axis=1)
        other_weights = table[:, index_bricks[brick]].reshape(NC, 16, NEIGH, ATOMS_DEV)
        own_weights = reduced_bricks[brick].reshape(NC, 16, 1, ATOMS_DEV)
        return pair_forces(separation, pair_mask, own_weights, other_weights)
    force_bricks, virial_bricks = lax.map(second_pass, brick_ids)
    alive_bricks = (jnp.arange(ATOMS_DEV)[None, :] < brick_count[:, None]).astype(jnp.float32)
    alive = alive_bricks.reshape(-1)
    forces = jnp.transpose(force_bricks, (1, 0, 2)).reshape(3, ATOMS)
    kicked = velocities + KICK * forces
    cell_ids = (brick_ids[:, None] * cell_total + atom_cell.reshape(brick_total, ATOMS_DEV)).reshape(-1)
    kinetic = jax.ops.segment_sum(alive * lax.optimization_barrier(jnp.sum(kicked * kicked, axis=0)), cell_ids, num_segments=brick_total * cell_total)
    filled = jax.ops.segment_sum(alive, cell_ids, num_segments=brick_total * cell_total)
    lattice = to_grid(kinetic / (3.0 * jnp.maximum(filled, 1.0)))
    occupancy = to_grid(jnp.minimum(filled, 1.0))
    electron = diffuse(electron_temp, conductivity, heating, lattice, occupancy)
    exchange_rate = RELAX * (electron - lattice) / (electron + lattice)
    per_atom = jnp.take_along_axis(from_grid(exchange_rate), atom_cell.reshape(brick_total, ATOMS_DEV), axis=1).reshape(-1)
    new_velocity = kicked * (1.0 + per_atom) * alive
    live_total = jnp.sum(brick_count).astype(jnp.float32)
    energy_total = jnp.sum(energies * alive_bricks)
    virial = lax.optimization_barrier(jnp.sum(virial_bricks, axis=0))
    totals = jnp.concatenate([jnp.reshape(energy_total, (1,)), virial.reshape(9)]) / live_total
    return (forces, new_velocity, electron, totals)
```

```python
import functools

import jax
import jax.numpy as jnp
from jax import lax
from jax.sharding import Mesh
from jax.sharding import PartitionSpec as P

SUBSTEPS = 4
GX_GY_GZ = ("gx_0", "gx_1", "gy_0", "gy_1", "gz")
GX = ("gx_0", "gx_1")
GY = ("gy_0", "gy_1")


HEAT_STEP = 0.15
COUPLE = 0.5
RELAX = 0.2
KICK = 0.05
SPREAD = 2.0
ROOT_THREE = 1.7320508


def padded(cells, sides, width):
    for axis, dim in sides:
        count = lax.axis_size(axis)
        head = lax.slice_in_dim(cells, 0, width, axis=dim)
        tail = lax.slice_in_dim(cells, cells.shape[dim] - width, cells.shape[dim], axis=dim)
        cells = jnp.concatenate(
            [
                lax.ppermute(tail, axis, [(i, (i + 1) % count) for i in range(count)]),
                cells,
                lax.ppermute(head, axis, [((i + 1) % count, i) for i in range(count)]),
            ],
            axis=dim,
        )
    return cells


def by_axis(shard, axes):
    return functools.reduce(lax.psum, axes, shard)


def column_gather(table, index):
    rows, width = table.shape
    lanes = 128
    blocks = -(-width // lanes)
    padded_table = jnp.pad(table, ((0, 0), (0, blocks * lanes - width)))
    flat = index.reshape(-1)
    high = flat // lanes
    low = flat % lanes
    picks = (jnp.arange(lanes)[:, None] == low[None, :]).astype(jnp.float32)
    spread = jnp.dot(
        padded_table.reshape(rows * blocks, lanes), picks, precision=lax.Precision.HIGHEST
    ).reshape(rows, blocks, flat.shape[0])
    chosen = jnp.arange(blocks)[:, None] == high[None, :]
    gathered = jnp.sum(jnp.where(chosen[None], spread, 0.0), axis=1)
    return gathered.reshape((rows,) + index.shape)


def harmonics(vector):
    coord_x, coord_y, coord_z = (vector[0], vector[1], vector[2])
    radius_sq = coord_x * coord_x + coord_y * coord_y + coord_z * coord_z
    terms = [
        jnp.ones_like(coord_x),
        coord_x,
        coord_y,
        coord_z,
        ROOT_THREE * coord_x * coord_y,
        ROOT_THREE * coord_y * coord_z,
        0.5 * (3.0 * coord_z * coord_z - radius_sq),
        ROOT_THREE * coord_x * coord_z,
        0.5 * ROOT_THREE * (coord_x * coord_x - coord_y * coord_y),
        0.79 * coord_y * (3.0 * coord_x * coord_x - coord_y * coord_y),
        3.87 * coord_x * coord_y * coord_z,
        0.61 * coord_y * (4.0 * coord_z * coord_z - coord_x * coord_x - coord_y * coord_y),
        0.5
        * coord_z
        * (2.0 * coord_z * coord_z - 3.0 * coord_x * coord_x - 3.0 * coord_y * coord_y),
        0.61 * coord_x * (4.0 * coord_z * coord_z - coord_x * coord_x - coord_y * coord_y),
        1.94 * coord_z * (coord_x * coord_x - coord_y * coord_y),
        0.79 * coord_x * (coord_x * coord_x - 3.0 * coord_y * coord_y),
    ]
    return jnp.stack(terms)


def radial(vector, orders):
    radius_sq = jnp.sum(vector * vector, axis=0)
    decay = jnp.exp(-radius_sq / SPREAD)
    argument = 2.0 * decay - 1.0
    polys = [jnp.ones_like(argument), argument]
    for order_id in range(2, orders):
        polys.append(2.0 * argument * polys[-1] - polys[-2])
    return decay * jnp.stack(polys[:orders])


def pair_energy(vector, weights):
    basis = radial(vector, weights.shape[0])
    mixed = jnp.sum(weights * basis[:, None], axis=0)
    return jnp.sum(mixed * harmonics(vector), axis=0)


def atom_basis(separation, pair_mask, radial_weight):
    basis = radial(separation, radial_weight.shape[1])
    shaped = (
        jnp.einsum("nc,cka->nka", radial_weight, basis, precision=lax.Precision.HIGHEST) * pair_mask
    )
    return jnp.einsum(
        "nka,mka->nma", shaped, harmonics(separation), precision=lax.Precision.HIGHEST
    )


def adjoints(basis_sum, linear_weight, pair_coupling):
    per_harmonic = jnp.concatenate(
        [
            jnp.repeat(pair_coupling[degree_id : degree_id + 1], copies, axis=0)
            for degree_id, copies in enumerate((1, 3, 5, 7))
        ],
        axis=0,
    )
    forward = jnp.einsum("mnp,pma->nma", per_harmonic, basis_sum, precision=lax.Precision.HIGHEST)
    backward = jnp.einsum("mpn,pma->nma", per_harmonic, basis_sum, precision=lax.Precision.HIGHEST)
    energy = jnp.dot(linear_weight, basis_sum[:, 0, :], precision=lax.Precision.HIGHEST) + jnp.sum(
        basis_sum * forward, axis=(0, 1)
    )
    isotropic = (jnp.arange(basis_sum.shape[1]) == 0).astype(jnp.float32)
    adjoint = forward + backward + linear_weight[:, None, None] * isotropic[None, :, None]
    return (energy, adjoint)


def pair_forces(separation, pair_mask, own_weights, other_weights):
    own_grad = jax.grad(lambda vector: jnp.sum(pair_energy(vector, own_weights)))(separation)
    other_grad = jax.grad(lambda vector: jnp.sum(pair_energy(vector, other_weights)))(-separation)
    pieces = (own_grad - other_grad) * pair_mask
    return (
        jnp.sum(pieces, axis=1),
        jnp.einsum("aki,bki->ab", separation, pieces, precision=lax.Precision.HIGHEST),
    )


def substep(temp_ext, kappa_ext, heat_here, lattice_here, occupancy_here, lower_open, upper_open):
    centre = temp_ext[1:-1, 1:-1, 1:-1]
    centre_kappa = kappa_ext[1:-1, 1:-1, 1:-1]

    def face(beside_temp, beside_kappa):
        return 0.5 * (centre_kappa + beside_kappa) * (beside_temp - centre)

    divergence = (
        face(temp_ext[1:-1, 1:-1, 2:], kappa_ext[1:-1, 1:-1, 2:])
        + face(temp_ext[1:-1, 1:-1, :-2], kappa_ext[1:-1, 1:-1, :-2])
        + face(temp_ext[1:-1, 2:, 1:-1], kappa_ext[1:-1, 2:, 1:-1])
        + face(temp_ext[1:-1, :-2, 1:-1], kappa_ext[1:-1, :-2, 1:-1])
        + face(temp_ext[2:, 1:-1, 1:-1], kappa_ext[2:, 1:-1, 1:-1]) * upper_open
        + face(temp_ext[:-2, 1:-1, 1:-1], kappa_ext[:-2, 1:-1, 1:-1]) * lower_open
    )
    return centre + HEAT_STEP / centre * (
        divergence + heat_here - COUPLE * occupancy_here * (centre - lattice_here)
    )


def local(
    positions,
    velocities,
    neighbour_index,
    neighbour_count,
    ghost_list,
    brick_count,
    atom_cell,
    radial_weight,
    linear_weight,
    pair_coupling,
    electron_temp,
    conductivity,
    heating,
):
    atom_slots = positions.shape[1]
    ghosts = ghost_list.shape[0]
    neigh_depth = neighbour_index.shape[0]
    orders = radial_weight.shape[1]
    live_count = brick_count[0]
    alive_mask = (jnp.arange(atom_slots) < live_count).astype(jnp.float32)
    slot_ids = jnp.arange(27)
    offsets = jnp.stack(
        [slot_ids // 9 - 1, slot_ids // 3 % 3 - 1, slot_ids % 3 - 1], axis=1
    ).astype(jnp.float32)
    ghost_sent = jnp.take(positions, ghost_list, axis=1).reshape(1, 1, 1, 3, ghosts)
    framed = padded(ghost_sent, ((GX, 0), (GY, 1), ("gz", 2)), 1)
    shifted = framed.reshape(27, 3, ghosts) + offsets[:, :, None]
    pos_table = jnp.concatenate(
        [positions, jnp.transpose(shifted, (1, 0, 2)).reshape(3, 27 * ghosts)], axis=1
    )
    separation = column_gather(pos_table, neighbour_index) - positions[:, None, :]
    pair_mask = (jnp.arange(neigh_depth)[:, None] < neighbour_count[None, :]).astype(jnp.float32)
    basis_sum = atom_basis(separation, pair_mask, radial_weight)
    energy, adjoint = adjoints(basis_sum, linear_weight, pair_coupling)
    reduced = jnp.einsum("nc,nma->cma", radial_weight, adjoint, precision=lax.Precision.HIGHEST)
    own_table = reduced.reshape(orders * 16, atom_slots)
    picked = jnp.take(own_table, ghost_list, axis=1).reshape(1, 1, 1, orders * 16, ghosts)
    framed_adjoint = padded(picked, ((GX, 0), (GY, 1), ("gz", 2)), 1)
    remote = framed_adjoint.reshape(27, orders * 16, ghosts)
    adjoint_table = jnp.concatenate(
        [own_table, jnp.transpose(remote, (1, 0, 2)).reshape(orders * 16, 27 * ghosts)], axis=1
    )
    other_weights = adjoint_table[:, neighbour_index].reshape(
        orders, 16, neigh_depth, atom_slots
    )
    forces, virial = pair_forces(
        separation, pair_mask, own_table.reshape(orders, 16, 1, atom_slots), other_weights
    )
    kicked = velocities + KICK * forces
    grid_shape = electron_temp.shape
    cell_total = grid_shape[0] * grid_shape[1] * grid_shape[2]
    kinetic = jax.ops.segment_sum(
        alive_mask * jnp.sum(kicked * kicked, axis=0), atom_cell, num_segments=cell_total
    )
    filled = jax.ops.segment_sum(alive_mask, atom_cell, num_segments=cell_total)
    lattice = (kinetic / (3.0 * jnp.maximum(filled, 1.0))).reshape(grid_shape)
    occupancy = jnp.minimum(filled, 1.0).reshape(grid_shape)
    depth_index = lax.axis_index("gz")
    depth_total = grid_shape[0] * lax.axis_size("gz")
    stacked = jnp.stack([electron_temp, conductivity, heating, lattice, occupancy])
    margins = padded(stacked, ((GX, 3), (GY, 2), ("gz", 1)), SUBSTEPS)
    electron = margins[0]
    cond_ext = margins[1]
    heat_ext = margins[2]
    lattice_ext = margins[3]
    occupancy_ext = margins[4]
    for substep_id in range(SUBSTEPS):
        margin = SUBSTEPS - substep_id - 1
        heat_ext = heat_ext[1:-1, 1:-1, 1:-1]
        lattice_ext = lattice_ext[1:-1, 1:-1, 1:-1]
        occupancy_ext = occupancy_ext[1:-1, 1:-1, 1:-1]
        global_z = depth_index * grid_shape[0] - margin + jnp.arange(heat_ext.shape[0])
        lower_open = (global_z != 0).astype(jnp.float32)[:, None, None]
        upper_open = (global_z != depth_total - 1).astype(jnp.float32)[:, None, None]
        lower_open, upper_open = (lower_open, upper_open)
        electron = substep(
            electron,
            cond_ext * electron,
            heat_ext,
            lattice_ext,
            occupancy_ext,
            lower_open,
            upper_open,
        )
        cond_ext = cond_ext[1:-1, 1:-1, 1:-1]
    exchange_rate = RELAX * (electron - lattice) / (electron + lattice)
    scaling = jnp.take(exchange_rate.reshape(-1), atom_cell)
    new_velocity = kicked * (1.0 + scaling) * alive_mask
    packed = jnp.concatenate(
        [
            jnp.reshape(jnp.sum(energy * alive_mask), (1,)),
            virial.reshape(9),
            jnp.reshape(live_count.astype(jnp.float32), (1,)),
        ]
    )
    summed = lax.psum(packed, GX_GY_GZ)
    totals = summed[:10] / summed[10]
    return (forces, new_velocity, electron, totals)


def solution(mesh):
    torus = Mesh(
        mesh.devices.reshape(2, 4, 8, 2, mesh.shape["gz"]), ("gx_0", "gx_1", "gy_0", "gy_1", "gz")
    )
    placed = (
        P(None, GX_GY_GZ),
        P(None, GX_GY_GZ),
        P(None, GX_GY_GZ),
        P(GX_GY_GZ),
        P(GX_GY_GZ),
        P(GX_GY_GZ),
        P(GX_GY_GZ),
        P(),
        P(),
        P(),
        P("gz", GY, GX),
        P("gz", GY, GX),
        P("gz", GY, GX),
    )
    return jax.shard_map(
        local,
        mesh=torus,
        in_specs=placed,
        out_specs=(P(None, GX_GY_GZ), P(None, GX_GY_GZ), P("gz", GY, GX), P()),
        check_vma=False,
    )
```

```python
import functools

import jax
import jax.numpy as jnp
from jax import lax
from jax.sharding import Mesh
from jax.sharding import PartitionSpec as P

SUBSTEPS = 4
GX_GY_GZ = ("gx_0", "gx_1", "gy_0", "gy_1", "gz")
GX = ("gx_0", "gx_1")
GY = ("gy_0", "gy_1")


HEAT_STEP = 0.15
COUPLE = 0.5
RELAX = 0.2
KICK = 0.05
SPREAD = 2.0
ROOT_THREE = 1.7320508


def padded(cells, sides, width):
    for axis, dim in sides:
        count = lax.axis_size(axis)
        head = lax.slice_in_dim(cells, 0, width, axis=dim)
        tail = lax.slice_in_dim(cells, cells.shape[dim] - width, cells.shape[dim], axis=dim)
        cells = jnp.concatenate(
            [
                lax.ppermute(tail, axis, [(i, (i + 1) % count) for i in range(count)]),
                cells,
                lax.ppermute(head, axis, [((i + 1) % count, i) for i in range(count)]),
            ],
            axis=dim,
        )
    return cells


def by_axis(shard, axes):
    return functools.reduce(lax.psum, axes, shard)


def group_sum(values, axes):
    count = lax.axis_size(axes)
    here = lax.axis_index(axes)
    received = [values] + [
        lax.ppermute(values, axes, [(j, (j - shift) % count) for j in range(count)])
        for shift in range(1, count)
    ]
    ordered = jnp.roll(jnp.stack(received), here, axis=0)
    return jnp.sum(ordered, axis=0)


def column_gather(table, index):
    rows, width = table.shape
    lanes = 128
    blocks = -(-width // lanes)
    padded_table = jnp.pad(table, ((0, 0), (0, blocks * lanes - width)))
    flat = index.reshape(-1)
    high = flat // lanes
    low = flat % lanes
    picks = (jnp.arange(lanes)[:, None] == low[None, :]).astype(jnp.float32)
    spread = jnp.dot(
        padded_table.reshape(rows * blocks, lanes), picks, precision=lax.Precision.HIGHEST
    ).reshape(rows, blocks, flat.shape[0])
    chosen = jnp.arange(blocks)[:, None] == high[None, :]
    gathered = jnp.sum(jnp.where(chosen[None], spread, 0.0), axis=1)
    return gathered.reshape((rows,) + index.shape)


def harmonics(vector):
    coord_x, coord_y, coord_z = (vector[0], vector[1], vector[2])
    radius_sq = coord_x * coord_x + coord_y * coord_y + coord_z * coord_z
    terms = [
        jnp.ones_like(coord_x),
        coord_x,
        coord_y,
        coord_z,
        ROOT_THREE * coord_x * coord_y,
        ROOT_THREE * coord_y * coord_z,
        0.5 * (3.0 * coord_z * coord_z - radius_sq),
        ROOT_THREE * coord_x * coord_z,
        0.5 * ROOT_THREE * (coord_x * coord_x - coord_y * coord_y),
        0.79 * coord_y * (3.0 * coord_x * coord_x - coord_y * coord_y),
        3.87 * coord_x * coord_y * coord_z,
        0.61 * coord_y * (4.0 * coord_z * coord_z - coord_x * coord_x - coord_y * coord_y),
        0.5
        * coord_z
        * (2.0 * coord_z * coord_z - 3.0 * coord_x * coord_x - 3.0 * coord_y * coord_y),
        0.61 * coord_x * (4.0 * coord_z * coord_z - coord_x * coord_x - coord_y * coord_y),
        1.94 * coord_z * (coord_x * coord_x - coord_y * coord_y),
        0.79 * coord_x * (coord_x * coord_x - 3.0 * coord_y * coord_y),
    ]
    return jnp.stack(terms)


def radial(vector, orders):
    radius_sq = jnp.sum(vector * vector, axis=0)
    decay = jnp.exp(-radius_sq / SPREAD)
    argument = 2.0 * decay - 1.0
    polys = [jnp.ones_like(argument), argument]
    for order_id in range(2, orders):
        polys.append(2.0 * argument * polys[-1] - polys[-2])
    return decay * jnp.stack(polys[:orders])


def pair_energy(vector, weights):
    basis = radial(vector, weights.shape[0])
    mixed = jnp.sum(weights * basis[:, None], axis=0)
    return jnp.sum(mixed * harmonics(vector), axis=0)


def atom_basis(separation, pair_mask, radial_weight):
    basis = radial(separation, radial_weight.shape[1])
    shaped = (
        jnp.einsum("nc,cka->nka", radial_weight, basis, precision=lax.Precision.HIGHEST) * pair_mask
    )
    return jnp.einsum(
        "nka,mka->nma", shaped, harmonics(separation), precision=lax.Precision.HIGHEST
    )


def adjoints(basis_sum, linear_weight, pair_coupling):
    per_harmonic = jnp.concatenate(
        [
            jnp.repeat(pair_coupling[degree_id : degree_id + 1], copies, axis=0)
            for degree_id, copies in enumerate((1, 3, 5, 7))
        ],
        axis=0,
    )
    forward = jnp.einsum("mnp,pma->nma", per_harmonic, basis_sum, precision=lax.Precision.HIGHEST)
    backward = jnp.einsum("mpn,pma->nma", per_harmonic, basis_sum, precision=lax.Precision.HIGHEST)
    energy = jnp.dot(linear_weight, basis_sum[:, 0, :], precision=lax.Precision.HIGHEST) + jnp.sum(
        basis_sum * forward, axis=(0, 1)
    )
    isotropic = (jnp.arange(basis_sum.shape[1]) == 0).astype(jnp.float32)
    adjoint = forward + backward + linear_weight[:, None, None] * isotropic[None, :, None]
    return (energy, adjoint)


def pair_forces(separation, pair_mask, own_weights, other_weights):
    own_grad = jax.grad(lambda vector: jnp.sum(pair_energy(vector, own_weights)))(separation)
    other_grad = jax.grad(lambda vector: jnp.sum(pair_energy(vector, other_weights)))(-separation)
    pieces = (own_grad - other_grad) * pair_mask
    return (
        jnp.sum(pieces, axis=1),
        jnp.einsum("aki,bki->ab", separation, pieces, precision=lax.Precision.HIGHEST),
    )


def substep(temp_ext, kappa_ext, heat_here, lattice_here, occupancy_here, lower_open, upper_open):
    centre = temp_ext[1:-1, 1:-1, 1:-1]
    centre_kappa = kappa_ext[1:-1, 1:-1, 1:-1]

    def face(beside_temp, beside_kappa):
        return 0.5 * (centre_kappa + beside_kappa) * (beside_temp - centre)

    divergence = (
        face(temp_ext[1:-1, 1:-1, 2:], kappa_ext[1:-1, 1:-1, 2:])
        + face(temp_ext[1:-1, 1:-1, :-2], kappa_ext[1:-1, 1:-1, :-2])
        + face(temp_ext[1:-1, 2:, 1:-1], kappa_ext[1:-1, 2:, 1:-1])
        + face(temp_ext[1:-1, :-2, 1:-1], kappa_ext[1:-1, :-2, 1:-1])
        + face(temp_ext[2:, 1:-1, 1:-1], kappa_ext[2:, 1:-1, 1:-1]) * upper_open
        + face(temp_ext[:-2, 1:-1, 1:-1], kappa_ext[:-2, 1:-1, 1:-1]) * lower_open
    )
    return centre + HEAT_STEP / centre * (
        divergence + heat_here - COUPLE * occupancy_here * (centre - lattice_here)
    )


def local(
    positions,
    velocities,
    neighbour_index,
    neighbour_count,
    ghost_list,
    brick_count,
    atom_cell,
    radial_weight,
    linear_weight,
    pair_coupling,
    electron_temp,
    conductivity,
    heating,
):
    atom_slots = positions.shape[1]
    ghosts = ghost_list.shape[0]
    neigh_depth = neighbour_index.shape[0]
    orders = radial_weight.shape[1]
    live_count = brick_count[0]
    alive_mask = (jnp.arange(atom_slots) < live_count).astype(jnp.float32)
    slot_ids = jnp.arange(27)
    offsets = jnp.stack(
        [slot_ids // 9 - 1, slot_ids // 3 % 3 - 1, slot_ids % 3 - 1], axis=1
    ).astype(jnp.float32)
    ghost_sent = jnp.take(positions, ghost_list, axis=1).reshape(1, 1, 1, 3, ghosts)
    framed = padded(ghost_sent, ((GX, 0), (GY, 1), ("gz", 2)), 1)
    shifted = framed.reshape(27, 3, ghosts) + offsets[:, :, None]
    pos_table = jnp.concatenate(
        [positions, jnp.transpose(shifted, (1, 0, 2)).reshape(3, 27 * ghosts)], axis=1
    )
    separation = column_gather(pos_table, neighbour_index) - positions[:, None, :]
    pair_mask = (jnp.arange(neigh_depth)[:, None] < neighbour_count[None, :]).astype(jnp.float32)
    basis_sum = atom_basis(separation, pair_mask, radial_weight)
    energy, adjoint = adjoints(basis_sum, linear_weight, pair_coupling)
    reduced = jnp.einsum("nc,nma->cma", radial_weight, adjoint, precision=lax.Precision.HIGHEST)
    own_table = reduced.reshape(orders * 16, atom_slots)
    picked = jnp.take(own_table, ghost_list, axis=1).reshape(1, 1, 1, orders * 16, ghosts)
    framed_adjoint = padded(picked, ((GX, 0), (GY, 1), ("gz", 2)), 1)
    remote = framed_adjoint.reshape(27, orders * 16, ghosts)
    adjoint_table = jnp.concatenate(
        [own_table, jnp.transpose(remote, (1, 0, 2)).reshape(orders * 16, 27 * ghosts)], axis=1
    )
    other_weights = adjoint_table[:, neighbour_index].reshape(
        orders, 16, neigh_depth, atom_slots
    )
    forces, virial = pair_forces(
        separation, pair_mask, own_table.reshape(orders, 16, 1, atom_slots), other_weights
    )
    kicked = velocities + KICK * forces
    grid_shape = electron_temp.shape
    cell_total = grid_shape[0] * grid_shape[1] * grid_shape[2]
    kinetic = jax.ops.segment_sum(
        alive_mask * jnp.sum(kicked * kicked, axis=0), atom_cell, num_segments=cell_total
    )
    filled = jax.ops.segment_sum(alive_mask, atom_cell, num_segments=cell_total)
    lattice = (kinetic / (3.0 * jnp.maximum(filled, 1.0))).reshape(grid_shape)
    occupancy = jnp.minimum(filled, 1.0).reshape(grid_shape)
    depth_index = lax.axis_index("gz")
    depth_total = grid_shape[0] * lax.axis_size("gz")
    stacked = jnp.stack([electron_temp, conductivity, heating, lattice, occupancy])
    margins = padded(stacked, ((GX, 3), (GY, 2), ("gz", 1)), SUBSTEPS)
    electron = margins[0]
    cond_ext = margins[1]
    heat_ext = margins[2]
    lattice_ext = margins[3]
    occupancy_ext = margins[4]
    for substep_id in range(SUBSTEPS):
        margin = SUBSTEPS - substep_id - 1
        heat_ext = heat_ext[1:-1, 1:-1, 1:-1]
        lattice_ext = lattice_ext[1:-1, 1:-1, 1:-1]
        occupancy_ext = occupancy_ext[1:-1, 1:-1, 1:-1]
        global_z = depth_index * grid_shape[0] - margin + jnp.arange(heat_ext.shape[0])
        lower_open = (global_z != 0).astype(jnp.float32)[:, None, None]
        upper_open = (global_z != depth_total - 1).astype(jnp.float32)[:, None, None]
        lower_open, upper_open = (lower_open, upper_open)
        electron = substep(
            electron,
            cond_ext * electron,
            heat_ext,
            lattice_ext,
            occupancy_ext,
            lower_open,
            upper_open,
        )
        cond_ext = cond_ext[1:-1, 1:-1, 1:-1]
    exchange_rate = RELAX * (electron - lattice) / (electron + lattice)
    scaling = jnp.take(exchange_rate.reshape(-1), atom_cell)
    new_velocity = kicked * (1.0 + scaling) * alive_mask
    packed = jnp.concatenate(
        [
            jnp.reshape(jnp.sum(energy * alive_mask), (1,)),
            virial.reshape(9),
            jnp.reshape(live_count.astype(jnp.float32), (1,)),
        ]
    )
    summed = functools.reduce(group_sum, (GX, GY, "gz"), packed)
    totals = summed[:10] / summed[10]
    return (forces, new_velocity, electron, totals)


def solution(mesh):
    torus = Mesh(
        mesh.devices.reshape(2, 4, 8, 2, mesh.shape["gz"]), ("gx_0", "gx_1", "gy_0", "gy_1", "gz")
    )
    placed = (
        P(None, GX_GY_GZ),
        P(None, GX_GY_GZ),
        P(None, GX_GY_GZ),
        P(GX_GY_GZ),
        P(GX_GY_GZ),
        P(GX_GY_GZ),
        P(GX_GY_GZ),
        P(),
        P(),
        P(),
        P("gz", GY, GX),
        P("gz", GY, GX),
        P("gz", GY, GX),
    )
    return jax.shard_map(
        local,
        mesh=torus,
        in_specs=placed,
        out_specs=(P(None, GX_GY_GZ), P(None, GX_GY_GZ), P("gz", GY, GX), P()),
        check_vma=False,
    )
```

```python
import functools

import jax
import jax.numpy as jnp
from jax import lax
from jax.sharding import Mesh
from jax.sharding import PartitionSpec as P

SUBSTEPS = 4
GX_GY_GZ = ("gx_0", "gx_1", "gy_0", "gy_1", "gz")
GX = ("gx_0", "gx_1")
GY = ("gy_0", "gy_1")


HEAT_STEP = 0.15
COUPLE = 0.5
RELAX = 0.2
KICK = 0.05
SPREAD = 2.0
ROOT_THREE = 1.7320508


def padded(cells, sides, width):
    for axis, dim in sides:
        count = lax.axis_size(axis)
        head = lax.slice_in_dim(cells, 0, width, axis=dim)
        tail = lax.slice_in_dim(cells, cells.shape[dim] - width, cells.shape[dim], axis=dim)
        cells = jnp.concatenate(
            [
                lax.ppermute(tail, axis, [(i, (i + 1) % count) for i in range(count)]),
                cells,
                lax.ppermute(head, axis, [((i + 1) % count, i) for i in range(count)]),
            ],
            axis=dim,
        )
    return cells


def by_axis(shard, axes):
    return functools.reduce(lax.psum, axes, shard)


def group_sum(values, axes):
    count = lax.axis_size(axes)
    here = lax.axis_index(axes)
    received = [values] + [
        lax.ppermute(values, axes, [(j, (j - shift) % count) for j in range(count)])
        for shift in range(1, count)
    ]
    ordered = jnp.roll(jnp.stack(received), here, axis=0)
    return jnp.sum(ordered, axis=0)


def column_gather(table, index):
    rows, width = table.shape
    lanes = 128
    blocks = -(-width // lanes)
    padded_table = jnp.pad(table, ((0, 0), (0, blocks * lanes - width)))
    flat = index.reshape(-1)
    high = flat // lanes
    low = flat % lanes
    picks = (jnp.arange(lanes)[:, None] == low[None, :]).astype(jnp.float32)
    spread = jnp.dot(
        padded_table.reshape(rows * blocks, lanes), picks, precision=lax.Precision.HIGHEST
    ).reshape(rows, blocks, flat.shape[0])
    chosen = jnp.arange(blocks)[:, None] == high[None, :]
    gathered = jnp.sum(jnp.where(chosen[None], spread, 0.0), axis=1)
    return gathered.reshape((rows,) + index.shape)


def harmonics(vector):
    coord_x, coord_y, coord_z = (vector[0], vector[1], vector[2])
    radius_sq = coord_x * coord_x + coord_y * coord_y + coord_z * coord_z
    terms = [
        jnp.ones_like(coord_x),
        coord_x,
        coord_y,
        coord_z,
        ROOT_THREE * coord_x * coord_y,
        ROOT_THREE * coord_y * coord_z,
        0.5 * (3.0 * coord_z * coord_z - radius_sq),
        ROOT_THREE * coord_x * coord_z,
        0.5 * ROOT_THREE * (coord_x * coord_x - coord_y * coord_y),
        0.79 * coord_y * (3.0 * coord_x * coord_x - coord_y * coord_y),
        3.87 * coord_x * coord_y * coord_z,
        0.61 * coord_y * (4.0 * coord_z * coord_z - coord_x * coord_x - coord_y * coord_y),
        0.5
        * coord_z
        * (2.0 * coord_z * coord_z - 3.0 * coord_x * coord_x - 3.0 * coord_y * coord_y),
        0.61 * coord_x * (4.0 * coord_z * coord_z - coord_x * coord_x - coord_y * coord_y),
        1.94 * coord_z * (coord_x * coord_x - coord_y * coord_y),
        0.79 * coord_x * (coord_x * coord_x - 3.0 * coord_y * coord_y),
    ]
    return jnp.stack(terms)


def radial(vector, orders):
    radius_sq = jnp.sum(vector * vector, axis=0)
    decay = jnp.exp(-radius_sq / SPREAD)
    argument = 2.0 * decay - 1.0
    polys = [jnp.ones_like(argument), argument]
    for order_id in range(2, orders):
        polys.append(2.0 * argument * polys[-1] - polys[-2])
    return decay * jnp.stack(polys[:orders])


def pair_energy(vector, weights):
    basis = radial(vector, weights.shape[0])
    mixed = jnp.sum(weights * basis[:, None], axis=0)
    return jnp.sum(mixed * harmonics(vector), axis=0)


def atom_basis(separation, pair_mask, radial_weight):
    basis = radial(separation, radial_weight.shape[1])
    shaped = (
        jnp.einsum("nc,cka->nka", radial_weight, basis, precision=lax.Precision.HIGHEST) * pair_mask
    )
    return jnp.einsum(
        "nka,mka->nma", shaped, harmonics(separation), precision=lax.Precision.HIGHEST
    )


def adjoints(basis_sum, linear_weight, pair_coupling):
    per_harmonic = jnp.concatenate(
        [
            jnp.repeat(pair_coupling[degree_id : degree_id + 1], copies, axis=0)
            for degree_id, copies in enumerate((1, 3, 5, 7))
        ],
        axis=0,
    )
    forward = jnp.einsum("mnp,pma->nma", per_harmonic, basis_sum, precision=lax.Precision.HIGHEST)
    backward = jnp.einsum("mpn,pma->nma", per_harmonic, basis_sum, precision=lax.Precision.HIGHEST)
    energy = jnp.dot(linear_weight, basis_sum[:, 0, :], precision=lax.Precision.HIGHEST) + jnp.sum(
        basis_sum * forward, axis=(0, 1)
    )
    isotropic = (jnp.arange(basis_sum.shape[1]) == 0).astype(jnp.float32)
    adjoint = forward + backward + linear_weight[:, None, None] * isotropic[None, :, None]
    return (energy, adjoint)


def pair_forces(separation, pair_mask, own_weights, other_weights):
    own_grad = jax.grad(lambda vector: jnp.sum(pair_energy(vector, own_weights)))(separation)
    other_grad = jax.grad(lambda vector: jnp.sum(pair_energy(vector, other_weights)))(-separation)
    pieces = (own_grad - other_grad) * pair_mask
    return (
        jnp.sum(pieces, axis=1),
        jnp.einsum("aki,bki->ab", separation, pieces, precision=lax.Precision.HIGHEST),
    )


def substep(temp_ext, kappa_ext, heat_here, lattice_here, occupancy_here, lower_open, upper_open):
    centre = temp_ext[1:-1, 1:-1, 1:-1]
    centre_kappa = kappa_ext[1:-1, 1:-1, 1:-1]

    def face(beside_temp, beside_kappa):
        return 0.5 * (centre_kappa + beside_kappa) * (beside_temp - centre)

    divergence = (
        face(temp_ext[1:-1, 1:-1, 2:], kappa_ext[1:-1, 1:-1, 2:])
        + face(temp_ext[1:-1, 1:-1, :-2], kappa_ext[1:-1, 1:-1, :-2])
        + face(temp_ext[1:-1, 2:, 1:-1], kappa_ext[1:-1, 2:, 1:-1])
        + face(temp_ext[1:-1, :-2, 1:-1], kappa_ext[1:-1, :-2, 1:-1])
        + face(temp_ext[2:, 1:-1, 1:-1], kappa_ext[2:, 1:-1, 1:-1]) * upper_open
        + face(temp_ext[:-2, 1:-1, 1:-1], kappa_ext[:-2, 1:-1, 1:-1]) * lower_open
    )
    return centre + HEAT_STEP / centre * (
        divergence + heat_here - COUPLE * occupancy_here * (centre - lattice_here)
    )


def local(
    positions,
    velocities,
    neighbour_index,
    neighbour_count,
    ghost_list,
    brick_count,
    atom_cell,
    radial_weight,
    linear_weight,
    pair_coupling,
    electron_temp,
    conductivity,
    heating,
):
    atom_slots = positions.shape[1]
    ghosts = ghost_list.shape[0]
    neigh_depth = neighbour_index.shape[0]
    orders = radial_weight.shape[1]
    live_count = brick_count[0]
    alive_mask = (jnp.arange(atom_slots) < live_count).astype(jnp.float32)
    slot_ids = jnp.arange(27)
    offsets = jnp.stack(
        [slot_ids // 9 - 1, slot_ids // 3 % 3 - 1, slot_ids % 3 - 1], axis=1
    ).astype(jnp.float32)
    ghost_sent = jnp.take(positions, ghost_list, axis=1).reshape(1, 1, 1, 3, ghosts)
    framed = padded(ghost_sent, ((GX, 0), (GY, 1), ("gz", 2)), 1)
    shifted = framed.reshape(27, 3, ghosts) + offsets[:, :, None]
    pos_table = jnp.concatenate(
        [positions, jnp.transpose(shifted, (1, 0, 2)).reshape(3, 27 * ghosts)], axis=1
    )
    separation = column_gather(pos_table, neighbour_index) - positions[:, None, :]
    pair_mask = (jnp.arange(neigh_depth)[:, None] < neighbour_count[None, :]).astype(jnp.float32)
    basis_sum = atom_basis(separation, pair_mask, radial_weight)
    energy, adjoint = adjoints(basis_sum, linear_weight, pair_coupling)
    reduced = jnp.einsum("nc,nma->cma", radial_weight, adjoint, precision=lax.Precision.HIGHEST)
    own_table = reduced.reshape(orders * 16, atom_slots)
    picked = jnp.take(own_table, ghost_list, axis=1).reshape(1, 1, 1, orders * 16, ghosts)
    framed_adjoint = padded(picked, ((GX, 0), (GY, 1), ("gz", 2)), 1)
    remote = framed_adjoint.reshape(27, orders * 16, ghosts)
    adjoint_table = jnp.concatenate(
        [own_table, jnp.transpose(remote, (1, 0, 2)).reshape(orders * 16, 27 * ghosts)], axis=1
    )
    other_weights = adjoint_table[:, neighbour_index].reshape(
        orders, 16, neigh_depth, atom_slots
    )
    forces, virial = pair_forces(
        separation, pair_mask, own_table.reshape(orders, 16, 1, atom_slots), other_weights
    )
    kicked = velocities + KICK * forces
    grid_shape = electron_temp.shape
    cell_total = grid_shape[0] * grid_shape[1] * grid_shape[2]
    kinetic = jax.ops.segment_sum(
        alive_mask * jnp.sum(kicked * kicked, axis=0), atom_cell, num_segments=cell_total
    )
    filled = jax.ops.segment_sum(alive_mask, atom_cell, num_segments=cell_total)
    lattice = (kinetic / (3.0 * jnp.maximum(filled, 1.0))).reshape(grid_shape)
    occupancy = jnp.minimum(filled, 1.0).reshape(grid_shape)
    depth_index = lax.axis_index("gz")
    depth_total = grid_shape[0] * lax.axis_size("gz")
    stacked = jnp.stack([electron_temp, conductivity, heating, lattice, occupancy])
    margins = padded(stacked, ((GX, 3), (GY, 2), ("gz", 1)), SUBSTEPS)
    electron = margins[0]
    cond_ext = margins[1]
    heat_ext = margins[2]
    lattice_ext = margins[3]
    occupancy_ext = margins[4]
    for substep_id in range(SUBSTEPS):
        margin = SUBSTEPS - substep_id - 1
        heat_ext = heat_ext[1:-1, 1:-1, 1:-1]
        lattice_ext = lattice_ext[1:-1, 1:-1, 1:-1]
        occupancy_ext = occupancy_ext[1:-1, 1:-1, 1:-1]
        global_z = depth_index * grid_shape[0] - margin + jnp.arange(heat_ext.shape[0])
        lower_open = (global_z != 0).astype(jnp.float32)[:, None, None]
        upper_open = (global_z != depth_total - 1).astype(jnp.float32)[:, None, None]
        lower_open, upper_open = (lower_open, upper_open)
        electron = substep(
            electron,
            cond_ext * electron,
            heat_ext,
            lattice_ext,
            occupancy_ext,
            lower_open,
            upper_open,
        )
        cond_ext = cond_ext[1:-1, 1:-1, 1:-1]
    exchange_rate = RELAX * (electron - lattice) / (electron + lattice)
    scaling = jnp.take(exchange_rate.reshape(-1), atom_cell)
    new_velocity = kicked * (1.0 + scaling) * alive_mask
    packed = jnp.concatenate(
        [
            jnp.reshape(jnp.sum(energy * alive_mask), (1,)),
            virial.reshape(9),
            jnp.reshape(live_count.astype(jnp.float32), (1,)),
        ]
    )
    summed = by_axis(packed, GX_GY_GZ)
    totals = summed[:10] / summed[10]
    return (forces, new_velocity, electron, totals)


def solution(mesh):
    torus = Mesh(
        mesh.devices.reshape(2, 4, 8, 2, mesh.shape["gz"]), ("gx_0", "gx_1", "gy_0", "gy_1", "gz")
    )
    placed = (
        P(None, GX_GY_GZ),
        P(None, GX_GY_GZ),
        P(None, GX_GY_GZ),
        P(GX_GY_GZ),
        P(GX_GY_GZ),
        P(GX_GY_GZ),
        P(GX_GY_GZ),
        P(),
        P(),
        P(),
        P("gz", GY, GX),
        P("gz", GY, GX),
        P("gz", GY, GX),
    )
    return jax.shard_map(
        local,
        mesh=torus,
        in_specs=placed,
        out_specs=(P(None, GX_GY_GZ), P(None, GX_GY_GZ), P("gz", GY, GX), P()),
        check_vma=False,
    )
```

```python
import functools

import jax
import jax.numpy as jnp
from jax import lax
from jax.experimental import pallas as pl
from jax.experimental.pallas import tpu as pltpu
from jax.sharding import Mesh
from jax.sharding import PartitionSpec as P

SUBSTEPS = 4
GX_GY_GZ = ("gx_0", "gx_1", "gy_0", "gy_1", "gz")
GX = ("gx_0", "gx_1")
GY = ("gy_0", "gy_1")


HEAT_STEP = 0.15
COUPLE = 0.5
RELAX = 0.2
KICK = 0.05
SPREAD = 2.0
ROOT_THREE = 1.7320508


def padded(cells, sides, width):
    for axis, dim in sides:
        count = lax.axis_size(axis)
        head = lax.slice_in_dim(cells, 0, width, axis=dim)
        tail = lax.slice_in_dim(cells, cells.shape[dim] - width, cells.shape[dim], axis=dim)
        cells = jnp.concatenate(
            [
                lax.ppermute(tail, axis, [(i, (i + 1) % count) for i in range(count)]),
                cells,
                lax.ppermute(head, axis, [((i + 1) % count, i) for i in range(count)]),
            ],
            axis=dim,
        )
    return cells


def by_axis(shard, axes):
    return functools.reduce(lax.psum, axes, shard)


def group_sum(values, axes):
    count = lax.axis_size(axes)
    here = lax.axis_index(axes)
    received = [values] + [
        lax.ppermute(values, axes, [(j, (j - shift) % count) for j in range(count)])
        for shift in range(1, count)
    ]
    ordered = jnp.roll(jnp.stack(received), here, axis=0)
    return jnp.sum(ordered, axis=0)


def row_gather(table_rows, flat_index, chunk=1024):
    rows, width = table_rows.shape
    total = flat_index.shape[0]

    def kernel(index_ref, table_ref, out_ref, stage_ref):
        base = pl.program_id(0) * chunk

        def copy_rows(group, carry):
            first = pl.multiple_of(group * 8, 8)
            picked = [
                table_ref[pl.ds(index_ref[base + first + r], 1), :] for r in range(8)
            ]
            stage_ref[pl.ds(first, 8), :] = jnp.concatenate(picked, axis=0)
            return carry

        lax.fori_loop(0, chunk // 8, copy_rows, 0, unroll=4)
        for part in range(chunk // 128):
            out_ref[:, part * 128 : (part + 1) * 128] = stage_ref[
                part * 128 : (part + 1) * 128, :
            ].T

    return pl.pallas_call(
        kernel,
        out_shape=jax.ShapeDtypeStruct((width, total), table_rows.dtype),
        grid_spec=pltpu.PrefetchScalarGridSpec(
            num_scalar_prefetch=1,
            grid=(total // chunk,),
            in_specs=[pl.BlockSpec((rows, width), lambda i, index: (0, 0))],
            out_specs=pl.BlockSpec((width, chunk), lambda i, index: (0, i)),
            scratch_shapes=[pltpu.VMEM((chunk, width), table_rows.dtype)],
        ),
        cost_estimate=pl.CostEstimate(
            flops=0, transcendentals=0, bytes_accessed=4 * (rows * width + 2 * width * total)
        ),
    )(flat_index, table_rows)


def column_gather(table, index):
    rows, width = table.shape
    lanes = 128
    blocks = -(-width // lanes)
    padded_table = jnp.pad(table, ((0, 0), (0, blocks * lanes - width)))
    flat = index.reshape(-1)
    high = flat // lanes
    low = flat % lanes
    picks = (jnp.arange(lanes)[:, None] == low[None, :]).astype(jnp.float32)
    spread = jnp.dot(
        padded_table.reshape(rows * blocks, lanes), picks, precision=lax.Precision.HIGHEST
    ).reshape(rows, blocks, flat.shape[0])
    chosen = jnp.arange(blocks)[:, None] == high[None, :]
    gathered = jnp.sum(jnp.where(chosen[None], spread, 0.0), axis=1)
    return gathered.reshape((rows,) + index.shape)


def harmonics(vector):
    coord_x, coord_y, coord_z = (vector[0], vector[1], vector[2])
    radius_sq = coord_x * coord_x + coord_y * coord_y + coord_z * coord_z
    terms = [
        jnp.ones_like(coord_x),
        coord_x,
        coord_y,
        coord_z,
        ROOT_THREE * coord_x * coord_y,
        ROOT_THREE * coord_y * coord_z,
        0.5 * (3.0 * coord_z * coord_z - radius_sq),
        ROOT_THREE * coord_x * coord_z,
        0.5 * ROOT_THREE * (coord_x * coord_x - coord_y * coord_y),
        0.79 * coord_y * (3.0 * coord_x * coord_x - coord_y * coord_y),
        3.87 * coord_x * coord_y * coord_z,
        0.61 * coord_y * (4.0 * coord_z * coord_z - coord_x * coord_x - coord_y * coord_y),
        0.5
        * coord_z
        * (2.0 * coord_z * coord_z - 3.0 * coord_x * coord_x - 3.0 * coord_y * coord_y),
        0.61 * coord_x * (4.0 * coord_z * coord_z - coord_x * coord_x - coord_y * coord_y),
        1.94 * coord_z * (coord_x * coord_x - coord_y * coord_y),
        0.79 * coord_x * (coord_x * coord_x - 3.0 * coord_y * coord_y),
    ]
    return jnp.stack(terms)


def radial(vector, orders):
    radius_sq = jnp.sum(vector * vector, axis=0)
    decay = jnp.exp(-radius_sq / SPREAD)
    argument = 2.0 * decay - 1.0
    polys = [jnp.ones_like(argument), argument]
    for order_id in range(2, orders):
        polys.append(2.0 * argument * polys[-1] - polys[-2])
    return decay * jnp.stack(polys[:orders])


def pair_energy(vector, weights):
    basis = radial(vector, weights.shape[0])
    mixed = jnp.sum(weights * basis[:, None], axis=0)
    return jnp.sum(mixed * harmonics(vector), axis=0)


def atom_basis(separation, pair_mask, radial_weight):
    basis = radial(separation, radial_weight.shape[1])
    shaped = (
        jnp.einsum("nc,cka->nka", radial_weight, basis, precision=lax.Precision.HIGHEST) * pair_mask
    )
    return jnp.einsum(
        "nka,mka->nma", shaped, harmonics(separation), precision=lax.Precision.HIGHEST
    )


def adjoints(basis_sum, linear_weight, pair_coupling):
    per_harmonic = jnp.concatenate(
        [
            jnp.repeat(pair_coupling[degree_id : degree_id + 1], copies, axis=0)
            for degree_id, copies in enumerate((1, 3, 5, 7))
        ],
        axis=0,
    )
    forward = jnp.einsum("mnp,pma->nma", per_harmonic, basis_sum, precision=lax.Precision.HIGHEST)
    backward = jnp.einsum("mpn,pma->nma", per_harmonic, basis_sum, precision=lax.Precision.HIGHEST)
    energy = jnp.dot(linear_weight, basis_sum[:, 0, :], precision=lax.Precision.HIGHEST) + jnp.sum(
        basis_sum * forward, axis=(0, 1)
    )
    isotropic = (jnp.arange(basis_sum.shape[1]) == 0).astype(jnp.float32)
    adjoint = forward + backward + linear_weight[:, None, None] * isotropic[None, :, None]
    return (energy, adjoint)


def pair_forces(separation, pair_mask, own_weights, other_weights):
    own_grad = jax.grad(lambda vector: jnp.sum(pair_energy(vector, own_weights)))(separation)
    other_grad = jax.grad(lambda vector: jnp.sum(pair_energy(vector, other_weights)))(-separation)
    pieces = (own_grad - other_grad) * pair_mask
    return (
        jnp.sum(pieces, axis=1),
        jnp.einsum("aki,bki->ab", separation, pieces, precision=lax.Precision.HIGHEST),
    )


def substep(temp_ext, kappa_ext, heat_here, lattice_here, occupancy_here, lower_open, upper_open):
    centre = temp_ext[1:-1, 1:-1, 1:-1]
    centre_kappa = kappa_ext[1:-1, 1:-1, 1:-1]

    def face(beside_temp, beside_kappa):
        return 0.5 * (centre_kappa + beside_kappa) * (beside_temp - centre)

    divergence = (
        face(temp_ext[1:-1, 1:-1, 2:], kappa_ext[1:-1, 1:-1, 2:])
        + face(temp_ext[1:-1, 1:-1, :-2], kappa_ext[1:-1, 1:-1, :-2])
        + face(temp_ext[1:-1, 2:, 1:-1], kappa_ext[1:-1, 2:, 1:-1])
        + face(temp_ext[1:-1, :-2, 1:-1], kappa_ext[1:-1, :-2, 1:-1])
        + face(temp_ext[2:, 1:-1, 1:-1], kappa_ext[2:, 1:-1, 1:-1]) * upper_open
        + face(temp_ext[:-2, 1:-1, 1:-1], kappa_ext[:-2, 1:-1, 1:-1]) * lower_open
    )
    return centre + HEAT_STEP / centre * (
        divergence + heat_here - COUPLE * occupancy_here * (centre - lattice_here)
    )


def local(
    positions,
    velocities,
    neighbour_index,
    neighbour_count,
    ghost_list,
    brick_count,
    atom_cell,
    radial_weight,
    linear_weight,
    pair_coupling,
    electron_temp,
    conductivity,
    heating,
):
    atom_slots = positions.shape[1]
    ghosts = ghost_list.shape[0]
    neigh_depth = neighbour_index.shape[0]
    orders = radial_weight.shape[1]
    live_count = brick_count[0]
    alive_mask = (jnp.arange(atom_slots) < live_count).astype(jnp.float32)
    slot_ids = jnp.arange(27)
    offsets = jnp.stack(
        [slot_ids // 9 - 1, slot_ids // 3 % 3 - 1, slot_ids % 3 - 1], axis=1
    ).astype(jnp.float32)
    ghost_sent = jnp.take(positions, ghost_list, axis=1).reshape(1, 1, 1, 3, ghosts)
    framed = padded(ghost_sent, (("gz", 2), (GX, 0), (GY, 1)), 1)
    shifted = framed.reshape(27, 3, ghosts) + offsets[:, :, None]
    pos_table = jnp.concatenate(
        [positions, jnp.transpose(shifted, (1, 0, 2)).reshape(3, 27 * ghosts)], axis=1
    )
    separation = column_gather(pos_table, neighbour_index) - positions[:, None, :]
    pair_mask = (jnp.arange(neigh_depth)[:, None] < neighbour_count[None, :]).astype(jnp.float32)
    basis_sum = atom_basis(separation, pair_mask, radial_weight)
    energy, adjoint = adjoints(basis_sum, linear_weight, pair_coupling)
    reduced = jnp.einsum("nc,nma->cma", radial_weight, adjoint, precision=lax.Precision.HIGHEST)
    own_table = reduced.reshape(orders * 16, atom_slots)
    picked = jnp.take(own_table, ghost_list, axis=1).reshape(1, 1, 1, orders * 16, ghosts)
    framed_adjoint = padded(picked, (("gz", 2), (GX, 0), (GY, 1)), 1)
    remote = framed_adjoint.reshape(27, orders * 16, ghosts)
    table_rows = jnp.concatenate(
        [own_table.T, jnp.transpose(remote, (0, 2, 1)).reshape(27 * ghosts, orders * 16)], axis=0
    )
    other_weights = row_gather(table_rows, neighbour_index.reshape(-1)).reshape(
        orders, 16, neigh_depth, atom_slots
    )
    forces, virial = pair_forces(
        separation, pair_mask, own_table.reshape(orders, 16, 1, atom_slots), other_weights
    )
    kicked = velocities + KICK * forces
    grid_shape = electron_temp.shape
    cell_total = grid_shape[0] * grid_shape[1] * grid_shape[2]
    kinetic = jax.ops.segment_sum(
        alive_mask * jnp.sum(kicked * kicked, axis=0), atom_cell, num_segments=cell_total
    )
    filled = jax.ops.segment_sum(alive_mask, atom_cell, num_segments=cell_total)
    lattice = (kinetic / (3.0 * jnp.maximum(filled, 1.0))).reshape(grid_shape)
    occupancy = jnp.minimum(filled, 1.0).reshape(grid_shape)
    depth_index = lax.axis_index("gz")
    depth_total = grid_shape[0] * lax.axis_size("gz")
    stacked = jnp.stack([electron_temp, conductivity, heating, lattice, occupancy])
    margins = padded(stacked, (("gz", 1), (GX, 3), (GY, 2)), SUBSTEPS)
    electron = margins[0]
    cond_ext = margins[1]
    heat_ext = margins[2]
    lattice_ext = margins[3]
    occupancy_ext = margins[4]
    for substep_id in range(SUBSTEPS):
        margin = SUBSTEPS - substep_id - 1
        heat_ext = heat_ext[1:-1, 1:-1, 1:-1]
        lattice_ext = lattice_ext[1:-1, 1:-1, 1:-1]
        occupancy_ext = occupancy_ext[1:-1, 1:-1, 1:-1]
        global_z = depth_index * grid_shape[0] - margin + jnp.arange(heat_ext.shape[0])
        lower_open = (global_z != 0).astype(jnp.float32)[:, None, None]
        upper_open = (global_z != depth_total - 1).astype(jnp.float32)[:, None, None]
        lower_open, upper_open = (lower_open, upper_open)
        electron = substep(
            electron,
            cond_ext * electron,
            heat_ext,
            lattice_ext,
            occupancy_ext,
            lower_open,
            upper_open,
        )
        cond_ext = cond_ext[1:-1, 1:-1, 1:-1]
    exchange_rate = RELAX * (electron - lattice) / (electron + lattice)
    scaling = jnp.take(exchange_rate.reshape(-1), atom_cell)
    new_velocity = kicked * (1.0 + scaling) * alive_mask
    packed = jnp.concatenate(
        [
            jnp.reshape(jnp.sum(energy * alive_mask), (1,)),
            virial.reshape(9),
            jnp.reshape(live_count.astype(jnp.float32), (1,)),
        ]
    )
    summed = by_axis(packed, GX_GY_GZ)
    totals = summed[:10] / summed[10]
    return (forces, new_velocity, electron, totals)


def solution(mesh):
    torus = Mesh(
        mesh.devices.reshape(2, 4, 8, 2, mesh.shape["gz"]), ("gx_0", "gx_1", "gy_0", "gy_1", "gz")
    )
    placed = (
        P(None, GX_GY_GZ),
        P(None, GX_GY_GZ),
        P(None, GX_GY_GZ),
        P(GX_GY_GZ),
        P(GX_GY_GZ),
        P(GX_GY_GZ),
        P(GX_GY_GZ),
        P(),
        P(),
        P(),
        P("gz", GY, GX),
        P("gz", GY, GX),
        P("gz", GY, GX),
    )
    return jax.shard_map(
        local,
        mesh=torus,
        in_specs=placed,
        out_specs=(P(None, GX_GY_GZ), P(None, GX_GY_GZ), P("gz", GY, GX), P()),
        check_vma=False,
    )
```

```python
import functools

import jax
import jax.numpy as jnp
from jax import lax
from jax.experimental import pallas as pl
from jax.experimental.pallas import tpu as pltpu
from jax.sharding import Mesh
from jax.sharding import PartitionSpec as P

SUBSTEPS = 4
GX_GY_GZ = ("gx_0", "gx_1", "gy_0", "gy_1", "gz")
GX = ("gx_0", "gx_1")
GY = ("gy_0", "gy_1")


HEAT_STEP = 0.15
COUPLE = 0.5
RELAX = 0.2
KICK = 0.05
SPREAD = 2.0
ROOT_THREE = 1.7320508


def padded(cells, sides, width):
    for axis, dim in sides:
        count = lax.axis_size(axis)
        head = lax.slice_in_dim(cells, 0, width, axis=dim)
        tail = lax.slice_in_dim(cells, cells.shape[dim] - width, cells.shape[dim], axis=dim)
        cells = jnp.concatenate(
            [
                lax.ppermute(tail, axis, [(i, (i + 1) % count) for i in range(count)]),
                cells,
                lax.ppermute(head, axis, [((i + 1) % count, i) for i in range(count)]),
            ],
            axis=dim,
        )
    return cells


def by_axis(shard, axes):
    return functools.reduce(lax.psum, axes, shard)


def group_sum(values, axes):
    count = lax.axis_size(axes)
    here = lax.axis_index(axes)
    received = [values] + [
        lax.ppermute(values, axes, [(j, (j - shift) % count) for j in range(count)])
        for shift in range(1, count)
    ]
    ordered = jnp.roll(jnp.stack(received), here, axis=0)
    return jnp.sum(ordered, axis=0)


def row_gather(table_rows, flat_index, chunk=1024):
    rows, width = table_rows.shape
    total = flat_index.shape[0]

    def kernel(index_ref, table_ref, out_ref, stage_ref):
        base = pl.program_id(0) * chunk

        def copy_rows(group, carry):
            first = pl.multiple_of(group * 8, 8)
            picked = [
                table_ref[pl.ds(index_ref[base + first + r], 1), :] for r in range(8)
            ]
            stage_ref[pl.ds(first, 8), :] = jnp.concatenate(picked, axis=0)
            return carry

        lax.fori_loop(0, chunk // 8, copy_rows, 0, unroll=4)
        for part in range(chunk // 128):
            out_ref[:, part * 128 : (part + 1) * 128] = stage_ref[
                part * 128 : (part + 1) * 128, :
            ].T

    return pl.pallas_call(
        kernel,
        out_shape=jax.ShapeDtypeStruct((width, total), table_rows.dtype),
        grid_spec=pltpu.PrefetchScalarGridSpec(
            num_scalar_prefetch=1,
            grid=(total // chunk,),
            in_specs=[pl.BlockSpec((rows, width), lambda i, index: (0, 0))],
            out_specs=pl.BlockSpec((width, chunk), lambda i, index: (0, i)),
            scratch_shapes=[pltpu.VMEM((chunk, width), table_rows.dtype)],
        ),
        cost_estimate=pl.CostEstimate(
            flops=0, transcendentals=0, bytes_accessed=4 * (rows * width + 2 * width * total)
        ),
    )(flat_index, table_rows)


def column_gather(table, index):
    rows, width = table.shape
    lanes = 128
    blocks = -(-width // lanes)
    padded_table = jnp.pad(table, ((0, 0), (0, blocks * lanes - width)))
    flat = index.reshape(-1)
    high = flat // lanes
    low = flat % lanes
    picks = (jnp.arange(lanes)[:, None] == low[None, :]).astype(jnp.float32)
    spread = jnp.dot(
        padded_table.reshape(rows * blocks, lanes), picks, precision=lax.Precision.HIGHEST
    ).reshape(rows, blocks, flat.shape[0])
    chosen = jnp.arange(blocks)[:, None] == high[None, :]
    gathered = jnp.sum(jnp.where(chosen[None], spread, 0.0), axis=1)
    return gathered.reshape((rows,) + index.shape)


def harmonics(vector):
    coord_x, coord_y, coord_z = (vector[0], vector[1], vector[2])
    radius_sq = coord_x * coord_x + coord_y * coord_y + coord_z * coord_z
    terms = [
        jnp.ones_like(coord_x),
        coord_x,
        coord_y,
        coord_z,
        ROOT_THREE * coord_x * coord_y,
        ROOT_THREE * coord_y * coord_z,
        0.5 * (3.0 * coord_z * coord_z - radius_sq),
        ROOT_THREE * coord_x * coord_z,
        0.5 * ROOT_THREE * (coord_x * coord_x - coord_y * coord_y),
        0.79 * coord_y * (3.0 * coord_x * coord_x - coord_y * coord_y),
        3.87 * coord_x * coord_y * coord_z,
        0.61 * coord_y * (4.0 * coord_z * coord_z - coord_x * coord_x - coord_y * coord_y),
        0.5
        * coord_z
        * (2.0 * coord_z * coord_z - 3.0 * coord_x * coord_x - 3.0 * coord_y * coord_y),
        0.61 * coord_x * (4.0 * coord_z * coord_z - coord_x * coord_x - coord_y * coord_y),
        1.94 * coord_z * (coord_x * coord_x - coord_y * coord_y),
        0.79 * coord_x * (coord_x * coord_x - 3.0 * coord_y * coord_y),
    ]
    return jnp.stack(terms)


def radial(vector, orders):
    radius_sq = jnp.sum(vector * vector, axis=0)
    decay = jnp.exp(-radius_sq / SPREAD)
    argument = 2.0 * decay - 1.0
    polys = [jnp.ones_like(argument), argument]
    for order_id in range(2, orders):
        polys.append(2.0 * argument * polys[-1] - polys[-2])
    return decay * jnp.stack(polys[:orders])


def pair_energy(vector, weights):
    basis = radial(vector, weights.shape[0])
    mixed = jnp.sum(weights * basis[:, None], axis=0)
    return jnp.sum(mixed * harmonics(vector), axis=0)


def atom_basis(separation, pair_mask, radial_weight):
    basis = radial(separation, radial_weight.shape[1])
    shaped = jnp.sum(radial_weight[:, :, None, None] * basis[None], axis=1) * pair_mask
    return jnp.sum(shaped[:, None] * harmonics(separation)[None], axis=2)


def adjoints(basis_sum, linear_weight, pair_coupling):
    per_harmonic = jnp.concatenate(
        [
            jnp.repeat(pair_coupling[degree_id : degree_id + 1], copies, axis=0)
            for degree_id, copies in enumerate((1, 3, 5, 7))
        ],
        axis=0,
    )
    by_harmonic = jnp.transpose(basis_sum, (1, 0, 2))
    forward = jnp.sum(
        jnp.transpose(per_harmonic, (1, 0, 2))[:, :, :, None] * by_harmonic[None], axis=2
    )
    backward = jnp.sum(
        jnp.transpose(per_harmonic, (2, 0, 1))[:, :, :, None] * by_harmonic[None], axis=2
    )
    energy = jnp.dot(linear_weight, basis_sum[:, 0, :], precision=lax.Precision.HIGHEST) + jnp.sum(
        basis_sum * forward, axis=(0, 1)
    )
    isotropic = (jnp.arange(basis_sum.shape[1]) == 0).astype(jnp.float32)
    adjoint = forward + backward + linear_weight[:, None, None] * isotropic[None, :, None]
    return (energy, adjoint)


def pair_forces(separation, pair_mask, own_weights, other_weights):
    own_grad = jax.grad(lambda vector: jnp.sum(pair_energy(vector, own_weights)))(separation)
    other_grad = jax.grad(lambda vector: jnp.sum(pair_energy(vector, other_weights)))(-separation)
    pieces = (own_grad - other_grad) * pair_mask
    return (
        jnp.sum(pieces, axis=1),
        jnp.einsum("aki,bki->ab", separation, pieces, precision=lax.Precision.HIGHEST),
    )


def substep(temp_ext, kappa_ext, heat_here, lattice_here, occupancy_here, lower_open, upper_open):
    centre = temp_ext[1:-1, 1:-1, 1:-1]
    centre_kappa = kappa_ext[1:-1, 1:-1, 1:-1]

    def face(beside_temp, beside_kappa):
        return 0.5 * (centre_kappa + beside_kappa) * (beside_temp - centre)

    divergence = (
        face(temp_ext[1:-1, 1:-1, 2:], kappa_ext[1:-1, 1:-1, 2:])
        + face(temp_ext[1:-1, 1:-1, :-2], kappa_ext[1:-1, 1:-1, :-2])
        + face(temp_ext[1:-1, 2:, 1:-1], kappa_ext[1:-1, 2:, 1:-1])
        + face(temp_ext[1:-1, :-2, 1:-1], kappa_ext[1:-1, :-2, 1:-1])
        + face(temp_ext[2:, 1:-1, 1:-1], kappa_ext[2:, 1:-1, 1:-1]) * upper_open
        + face(temp_ext[:-2, 1:-1, 1:-1], kappa_ext[:-2, 1:-1, 1:-1]) * lower_open
    )
    return centre + HEAT_STEP / centre * (
        divergence + heat_here - COUPLE * occupancy_here * (centre - lattice_here)
    )


def local(
    positions,
    velocities,
    neighbour_index,
    neighbour_count,
    ghost_list,
    brick_count,
    atom_cell,
    radial_weight,
    linear_weight,
    pair_coupling,
    electron_temp,
    conductivity,
    heating,
):
    atom_slots = positions.shape[1]
    ghosts = ghost_list.shape[0]
    neigh_depth = neighbour_index.shape[0]
    orders = radial_weight.shape[1]
    live_count = brick_count[0]
    alive_mask = (jnp.arange(atom_slots) < live_count).astype(jnp.float32)
    slot_ids = jnp.arange(27)
    offsets = jnp.stack(
        [slot_ids // 9 - 1, slot_ids // 3 % 3 - 1, slot_ids % 3 - 1], axis=1
    ).astype(jnp.float32)
    ghost_sent = jnp.take(positions, ghost_list, axis=1).reshape(1, 1, 1, 3, ghosts)
    framed = padded(ghost_sent, (("gz", 2), (GX, 0), (GY, 1)), 1)
    shifted = framed.reshape(27, 3, ghosts) + offsets[:, :, None]
    pos_table = jnp.concatenate(
        [positions, jnp.transpose(shifted, (1, 0, 2)).reshape(3, 27 * ghosts)], axis=1
    )
    separation = column_gather(pos_table, neighbour_index) - positions[:, None, :]
    pair_mask = (jnp.arange(neigh_depth)[:, None] < neighbour_count[None, :]).astype(jnp.float32)
    basis_sum = atom_basis(separation, pair_mask, radial_weight)
    energy, adjoint = adjoints(basis_sum, linear_weight, pair_coupling)
    reduced = jnp.sum(radial_weight.T[:, :, None, None] * adjoint[None], axis=1)
    own_table = reduced.reshape(orders * 16, atom_slots)
    picked = jnp.take(own_table, ghost_list, axis=1).reshape(1, 1, 1, orders * 16, ghosts)
    framed_adjoint = padded(picked, (("gz", 2), (GX, 0), (GY, 1)), 1)
    remote = framed_adjoint.reshape(27, orders * 16, ghosts)
    table_rows = jnp.concatenate(
        [own_table.T, jnp.transpose(remote, (0, 2, 1)).reshape(27 * ghosts, orders * 16)], axis=0
    )
    other_weights = row_gather(table_rows, neighbour_index.reshape(-1)).reshape(
        orders, 16, neigh_depth, atom_slots
    )
    forces, virial = pair_forces(
        separation, pair_mask, own_table.reshape(orders, 16, 1, atom_slots), other_weights
    )
    kicked = velocities + KICK * forces
    grid_shape = electron_temp.shape
    cell_total = grid_shape[0] * grid_shape[1] * grid_shape[2]
    cell_picks = (jnp.arange(cell_total)[:, None] == atom_cell[None, :]).astype(jnp.float32)
    per_cell = jnp.dot(
        cell_picks,
        jnp.stack([alive_mask * jnp.sum(kicked * kicked, axis=0), alive_mask], axis=1),
        precision=lax.Precision.HIGHEST,
    )
    kinetic = per_cell[:, 0]
    filled = per_cell[:, 1]
    lattice = (kinetic / (3.0 * jnp.maximum(filled, 1.0))).reshape(grid_shape)
    occupancy = jnp.minimum(filled, 1.0).reshape(grid_shape)
    depth_index = lax.axis_index("gz")
    depth_total = grid_shape[0] * lax.axis_size("gz")
    stacked = jnp.stack([electron_temp, conductivity, heating, lattice, occupancy])
    margins = padded(stacked, (("gz", 1), (GX, 3), (GY, 2)), SUBSTEPS)
    electron = margins[0]
    cond_ext = margins[1]
    heat_ext = margins[2]
    lattice_ext = margins[3]
    occupancy_ext = margins[4]
    for substep_id in range(SUBSTEPS):
        margin = SUBSTEPS - substep_id - 1
        heat_ext = heat_ext[1:-1, 1:-1, 1:-1]
        lattice_ext = lattice_ext[1:-1, 1:-1, 1:-1]
        occupancy_ext = occupancy_ext[1:-1, 1:-1, 1:-1]
        global_z = depth_index * grid_shape[0] - margin + jnp.arange(heat_ext.shape[0])
        lower_open = (global_z != 0).astype(jnp.float32)[:, None, None]
        upper_open = (global_z != depth_total - 1).astype(jnp.float32)[:, None, None]
        lower_open, upper_open = (lower_open, upper_open)
        electron = substep(
            electron,
            cond_ext * electron,
            heat_ext,
            lattice_ext,
            occupancy_ext,
            lower_open,
            upper_open,
        )
        cond_ext = cond_ext[1:-1, 1:-1, 1:-1]
    exchange_rate = RELAX * (electron - lattice) / (electron + lattice)
    scaling = jnp.dot(
        exchange_rate.reshape(1, -1), cell_picks, precision=lax.Precision.HIGHEST
    ).reshape(-1)
    new_velocity = kicked * (1.0 + scaling) * alive_mask
    packed = jnp.concatenate(
        [
            jnp.reshape(jnp.sum(energy * alive_mask), (1,)),
            virial.reshape(9),
            jnp.reshape(live_count.astype(jnp.float32), (1,)),
        ]
    )
    summed = by_axis(packed, GX_GY_GZ)
    totals = summed[:10] / summed[10]
    return (forces, new_velocity, electron, totals)


def solution(mesh):
    torus = Mesh(
        mesh.devices.reshape(2, 4, 8, 2, mesh.shape["gz"]), ("gx_0", "gx_1", "gy_0", "gy_1", "gz")
    )
    placed = (
        P(None, GX_GY_GZ),
        P(None, GX_GY_GZ),
        P(None, GX_GY_GZ),
        P(GX_GY_GZ),
        P(GX_GY_GZ),
        P(GX_GY_GZ),
        P(GX_GY_GZ),
        P(),
        P(),
        P(),
        P("gz", GY, GX),
        P("gz", GY, GX),
        P("gz", GY, GX),
    )
    return jax.shard_map(
        local,
        mesh=torus,
        in_specs=placed,
        out_specs=(P(None, GX_GY_GZ), P(None, GX_GY_GZ), P("gz", GY, GX), P()),
        check_vma=False,
    )
```

```python
import functools

import jax
import jax.numpy as jnp
from jax import lax
from jax.experimental import pallas as pl
from jax.experimental.pallas import tpu as pltpu
from jax.sharding import Mesh
from jax.sharding import PartitionSpec as P

SUBSTEPS = 4
GX_GY_GZ = ("gx_0", "gx_1", "gy_0", "gy_1", "gz")
GX = ("gx_0", "gx_1")
GY = ("gy_0", "gy_1")


HEAT_STEP = 0.15
COUPLE = 0.5
RELAX = 0.2
KICK = 0.05
SPREAD = 2.0
ROOT_THREE = 1.7320508


def padded(cells, sides, width):
    for axis, dim in sides:
        count = lax.axis_size(axis)
        head = lax.slice_in_dim(cells, 0, width, axis=dim)
        tail = lax.slice_in_dim(cells, cells.shape[dim] - width, cells.shape[dim], axis=dim)
        cells = jnp.concatenate(
            [
                lax.ppermute(tail, axis, [(i, (i + 1) % count) for i in range(count)]),
                cells,
                lax.ppermute(head, axis, [((i + 1) % count, i) for i in range(count)]),
            ],
            axis=dim,
        )
    return cells


def by_axis(shard, axes):
    return functools.reduce(lax.psum, axes, shard)


def group_sum(values, axes):
    count = lax.axis_size(axes)
    here = lax.axis_index(axes)
    received = [values] + [
        lax.ppermute(values, axes, [(j, (j - shift) % count) for j in range(count)])
        for shift in range(1, count)
    ]
    ordered = jnp.roll(jnp.stack(received), here, axis=0)
    return jnp.sum(ordered, axis=0)


def row_gather(table_rows, flat_index, chunk=1024):
    rows, width = table_rows.shape
    total = flat_index.shape[0]

    def kernel(index_ref, table_ref, out_ref, stage_ref):
        base = pl.program_id(0) * chunk

        def copy_rows(group, carry):
            first = pl.multiple_of(group * 8, 8)
            picked = [
                table_ref[pl.ds(index_ref[base + first + r], 1), :] for r in range(8)
            ]
            stage_ref[pl.ds(first, 8), :] = jnp.concatenate(picked, axis=0)
            return carry

        lax.fori_loop(0, chunk // 8, copy_rows, 0, unroll=4)
        for part in range(chunk // 128):
            out_ref[:, part * 128 : (part + 1) * 128] = stage_ref[
                part * 128 : (part + 1) * 128, :
            ].T

    return pl.pallas_call(
        kernel,
        out_shape=jax.ShapeDtypeStruct((width, total), table_rows.dtype),
        grid_spec=pltpu.PrefetchScalarGridSpec(
            num_scalar_prefetch=1,
            grid=(total // chunk,),
            in_specs=[pl.BlockSpec((rows, width), lambda i, index: (0, 0))],
            out_specs=pl.BlockSpec((width, chunk), lambda i, index: (0, i)),
            scratch_shapes=[pltpu.VMEM((chunk, width), table_rows.dtype)],
        ),
        cost_estimate=pl.CostEstimate(
            flops=0, transcendentals=0, bytes_accessed=4 * (rows * width + 2 * width * total)
        ),
    )(flat_index, table_rows)


def column_gather(table, index):
    rows, width = table.shape
    lanes = 128
    blocks = -(-width // lanes)
    padded_table = jnp.pad(table, ((0, 0), (0, blocks * lanes - width)))
    flat = index.reshape(-1)
    high = flat // lanes
    low = flat % lanes
    picks = (jnp.arange(lanes)[:, None] == low[None, :]).astype(jnp.float32)
    spread = jnp.dot(
        padded_table.reshape(rows * blocks, lanes), picks, precision=lax.Precision.HIGHEST
    ).reshape(rows, blocks, flat.shape[0])
    chosen = jnp.arange(blocks)[:, None] == high[None, :]
    gathered = jnp.sum(jnp.where(chosen[None], spread, 0.0), axis=1)
    return gathered.reshape((rows,) + index.shape)


def harmonics(vector):
    coord_x, coord_y, coord_z = (vector[0], vector[1], vector[2])
    radius_sq = coord_x * coord_x + coord_y * coord_y + coord_z * coord_z
    terms = [
        jnp.ones_like(coord_x),
        coord_x,
        coord_y,
        coord_z,
        ROOT_THREE * coord_x * coord_y,
        ROOT_THREE * coord_y * coord_z,
        0.5 * (3.0 * coord_z * coord_z - radius_sq),
        ROOT_THREE * coord_x * coord_z,
        0.5 * ROOT_THREE * (coord_x * coord_x - coord_y * coord_y),
        0.79 * coord_y * (3.0 * coord_x * coord_x - coord_y * coord_y),
        3.87 * coord_x * coord_y * coord_z,
        0.61 * coord_y * (4.0 * coord_z * coord_z - coord_x * coord_x - coord_y * coord_y),
        0.5
        * coord_z
        * (2.0 * coord_z * coord_z - 3.0 * coord_x * coord_x - 3.0 * coord_y * coord_y),
        0.61 * coord_x * (4.0 * coord_z * coord_z - coord_x * coord_x - coord_y * coord_y),
        1.94 * coord_z * (coord_x * coord_x - coord_y * coord_y),
        0.79 * coord_x * (coord_x * coord_x - 3.0 * coord_y * coord_y),
    ]
    return jnp.stack(terms)


def radial(vector, orders):
    radius_sq = jnp.sum(vector * vector, axis=0)
    decay = jnp.exp(-radius_sq / SPREAD)
    argument = 2.0 * decay - 1.0
    polys = [jnp.ones_like(argument), argument]
    for order_id in range(2, orders):
        polys.append(2.0 * argument * polys[-1] - polys[-2])
    return decay * jnp.stack(polys[:orders])


def pair_energy(vector, weights):
    basis = radial(vector, weights.shape[1])
    mixed = jnp.sum(weights * basis[None], axis=1)
    return jnp.sum(mixed * harmonics(vector), axis=0)


def atom_basis(separation, pair_mask, radial_weight):
    basis = radial(separation, radial_weight.shape[1])
    shaped = jnp.sum(radial_weight[:, :, None, None] * basis[None], axis=1) * pair_mask
    return jnp.sum(shaped[:, None] * harmonics(separation)[None], axis=2)


def adjoints(basis_sum, linear_weight, pair_coupling):
    per_harmonic = jnp.concatenate(
        [
            jnp.repeat(pair_coupling[degree_id : degree_id + 1], copies, axis=0)
            for degree_id, copies in enumerate((1, 3, 5, 7))
        ],
        axis=0,
    )
    by_harmonic = jnp.transpose(basis_sum, (1, 0, 2))
    forward = jnp.sum(
        jnp.transpose(per_harmonic, (1, 0, 2))[:, :, :, None] * by_harmonic[None], axis=2
    )
    backward = jnp.sum(
        jnp.transpose(per_harmonic, (2, 0, 1))[:, :, :, None] * by_harmonic[None], axis=2
    )
    energy = jnp.dot(linear_weight, basis_sum[:, 0, :], precision=lax.Precision.HIGHEST) + jnp.sum(
        basis_sum * forward, axis=(0, 1)
    )
    isotropic = (jnp.arange(basis_sum.shape[1]) == 0).astype(jnp.float32)
    adjoint = forward + backward + linear_weight[:, None, None] * isotropic[None, :, None]
    return (energy, adjoint)


def pair_forces(separation, pair_mask, own_weights, other_weights):
    own_grad = jax.grad(lambda vector: jnp.sum(pair_energy(vector, own_weights)))(separation)
    other_grad = jax.grad(lambda vector: jnp.sum(pair_energy(vector, other_weights)))(-separation)
    pieces = (own_grad - other_grad) * pair_mask
    return (
        jnp.sum(pieces, axis=1),
        jnp.einsum("aki,bki->ab", separation, pieces, precision=lax.Precision.HIGHEST),
    )


def substep(temp_ext, kappa_ext, heat_here, lattice_here, occupancy_here, lower_open, upper_open):
    centre = temp_ext[1:-1, 1:-1, 1:-1]
    centre_kappa = kappa_ext[1:-1, 1:-1, 1:-1]

    def face(beside_temp, beside_kappa):
        return 0.5 * (centre_kappa + beside_kappa) * (beside_temp - centre)

    divergence = (
        face(temp_ext[1:-1, 1:-1, 2:], kappa_ext[1:-1, 1:-1, 2:])
        + face(temp_ext[1:-1, 1:-1, :-2], kappa_ext[1:-1, 1:-1, :-2])
        + face(temp_ext[1:-1, 2:, 1:-1], kappa_ext[1:-1, 2:, 1:-1])
        + face(temp_ext[1:-1, :-2, 1:-1], kappa_ext[1:-1, :-2, 1:-1])
        + face(temp_ext[2:, 1:-1, 1:-1], kappa_ext[2:, 1:-1, 1:-1]) * upper_open
        + face(temp_ext[:-2, 1:-1, 1:-1], kappa_ext[:-2, 1:-1, 1:-1]) * lower_open
    )
    return centre + HEAT_STEP / centre * (
        divergence + heat_here - COUPLE * occupancy_here * (centre - lattice_here)
    )


def local(
    positions,
    velocities,
    neighbour_index,
    neighbour_count,
    ghost_list,
    brick_count,
    atom_cell,
    radial_weight,
    linear_weight,
    pair_coupling,
    electron_temp,
    conductivity,
    heating,
):
    atom_slots = positions.shape[1]
    ghosts = ghost_list.shape[0]
    neigh_depth = neighbour_index.shape[0]
    orders = radial_weight.shape[1]
    live_count = brick_count[0]
    alive_mask = (jnp.arange(atom_slots) < live_count).astype(jnp.float32)
    slot_ids = jnp.arange(27)
    offsets = jnp.stack(
        [slot_ids // 9 - 1, slot_ids // 3 % 3 - 1, slot_ids % 3 - 1], axis=1
    ).astype(jnp.float32)
    ghost_sent = jnp.take(positions, ghost_list, axis=1).reshape(1, 1, 1, 3, ghosts)
    framed = padded(ghost_sent, (("gz", 2), (GX, 0), (GY, 1)), 1)
    shifted = framed.reshape(27, 3, ghosts) + offsets[:, :, None]
    pos_table = jnp.concatenate(
        [positions, jnp.transpose(shifted, (1, 0, 2)).reshape(3, 27 * ghosts)], axis=1
    )
    separation = column_gather(pos_table, neighbour_index) - positions[:, None, :]
    pair_mask = (jnp.arange(neigh_depth)[:, None] < neighbour_count[None, :]).astype(jnp.float32)
    basis_sum = atom_basis(separation, pair_mask, radial_weight)
    energy, adjoint = adjoints(basis_sum, linear_weight, pair_coupling)
    reduced = jnp.sum(radial_weight.T[:, :, None, None] * adjoint[None], axis=1)
    own_table = jnp.transpose(reduced, (1, 0, 2)).reshape(16 * orders, atom_slots)
    picked = jnp.take(own_table, ghost_list, axis=1).reshape(1, 1, 1, orders * 16, ghosts)
    framed_adjoint = padded(picked, (("gz", 2), (GX, 0), (GY, 1)), 1)
    remote = framed_adjoint.reshape(27, orders * 16, ghosts)
    table_rows = jnp.concatenate(
        [own_table.T, jnp.transpose(remote, (0, 2, 1)).reshape(27 * ghosts, orders * 16)], axis=0
    )
    other_weights = row_gather(table_rows, neighbour_index.reshape(-1)).reshape(
        16, orders, neigh_depth, atom_slots
    )
    forces, virial = pair_forces(
        separation, pair_mask, own_table.reshape(16, orders, 1, atom_slots), other_weights
    )
    kicked = velocities + KICK * forces
    grid_shape = electron_temp.shape
    cell_total = grid_shape[0] * grid_shape[1] * grid_shape[2]
    cell_picks = (jnp.arange(cell_total)[:, None] == atom_cell[None, :]).astype(jnp.float32)
    per_cell = jnp.dot(
        cell_picks,
        jnp.stack([alive_mask * jnp.sum(kicked * kicked, axis=0), alive_mask], axis=1),
        precision=lax.Precision.HIGHEST,
    )
    kinetic = per_cell[:, 0]
    filled = per_cell[:, 1]
    lattice = (kinetic / (3.0 * jnp.maximum(filled, 1.0))).reshape(grid_shape)
    occupancy = jnp.minimum(filled, 1.0).reshape(grid_shape)
    depth_index = lax.axis_index("gz")
    depth_total = grid_shape[0] * lax.axis_size("gz")
    stacked = jnp.stack([electron_temp, conductivity, heating, lattice, occupancy])
    margins = padded(stacked, (("gz", 1), (GX, 3), (GY, 2)), SUBSTEPS)
    electron = margins[0]
    cond_ext = margins[1]
    heat_ext = margins[2]
    lattice_ext = margins[3]
    occupancy_ext = margins[4]
    for substep_id in range(SUBSTEPS):
        margin = SUBSTEPS - substep_id - 1
        heat_ext = heat_ext[1:-1, 1:-1, 1:-1]
        lattice_ext = lattice_ext[1:-1, 1:-1, 1:-1]
        occupancy_ext = occupancy_ext[1:-1, 1:-1, 1:-1]
        global_z = depth_index * grid_shape[0] - margin + jnp.arange(heat_ext.shape[0])
        lower_open = (global_z != 0).astype(jnp.float32)[:, None, None]
        upper_open = (global_z != depth_total - 1).astype(jnp.float32)[:, None, None]
        lower_open, upper_open = (lower_open, upper_open)
        electron = substep(
            electron,
            cond_ext * electron,
            heat_ext,
            lattice_ext,
            occupancy_ext,
            lower_open,
            upper_open,
        )
        cond_ext = cond_ext[1:-1, 1:-1, 1:-1]
    exchange_rate = RELAX * (electron - lattice) / (electron + lattice)
    scaling = jnp.dot(
        exchange_rate.reshape(1, -1), cell_picks, precision=lax.Precision.HIGHEST
    ).reshape(-1)
    new_velocity = kicked * (1.0 + scaling) * alive_mask
    packed = jnp.concatenate(
        [
            jnp.reshape(jnp.sum(energy * alive_mask), (1,)),
            virial.reshape(9),
            jnp.reshape(live_count.astype(jnp.float32), (1,)),
        ]
    )
    summed = by_axis(packed, GX_GY_GZ)
    totals = summed[:10] / summed[10]
    return (forces, new_velocity, electron, totals)


def solution(mesh):
    torus = Mesh(
        mesh.devices.reshape(2, 4, 8, 2, mesh.shape["gz"]), ("gx_0", "gx_1", "gy_0", "gy_1", "gz")
    )
    placed = (
        P(None, GX_GY_GZ),
        P(None, GX_GY_GZ),
        P(None, GX_GY_GZ),
        P(GX_GY_GZ),
        P(GX_GY_GZ),
        P(GX_GY_GZ),
        P(GX_GY_GZ),
        P(),
        P(),
        P(),
        P("gz", GY, GX),
        P("gz", GY, GX),
        P("gz", GY, GX),
    )
    return jax.shard_map(
        local,
        mesh=torus,
        in_specs=placed,
        out_specs=(P(None, GX_GY_GZ), P(None, GX_GY_GZ), P("gz", GY, GX), P()),
        check_vma=False,
    )
```

```python
import functools

import jax
import jax.numpy as jnp
from jax import lax
from jax.experimental import pallas as pl
from jax.experimental.pallas import tpu as pltpu
from jax.sharding import Mesh
from jax.sharding import PartitionSpec as P

SUBSTEPS = 4
GX_GY_GZ = ("gx_0", "gx_1", "gy_0", "gy_1", "gz")
GX = ("gx_0", "gx_1")
GY = ("gy_0", "gy_1")


HEAT_STEP = 0.15
COUPLE = 0.5
RELAX = 0.2
KICK = 0.05
SPREAD = 2.0
ROOT_THREE = 1.7320508


def padded(cells, sides, width, open_axes=()):
    for axis, dim in sides:
        count = lax.axis_size(axis)
        links = count if axis not in open_axes else count - 1
        head = lax.slice_in_dim(cells, 0, width, axis=dim)
        tail = lax.slice_in_dim(cells, cells.shape[dim] - width, cells.shape[dim], axis=dim)
        cells = jnp.concatenate(
            [
                lax.ppermute(tail, axis, [(i, (i + 1) % count) for i in range(links)]),
                cells,
                lax.ppermute(head, axis, [((i + 1) % count, i) for i in range(links)]),
            ],
            axis=dim,
        )
    return cells


def by_axis(shard, axes):
    return functools.reduce(lax.psum, axes, shard)


def group_sum(values, axes):
    count = lax.axis_size(axes)
    here = lax.axis_index(axes)
    received = [values] + [
        lax.ppermute(values, axes, [(j, (j - shift) % count) for j in range(count)])
        for shift in range(1, count)
    ]
    ordered = jnp.roll(jnp.stack(received), here, axis=0)
    return jnp.sum(ordered, axis=0)


def row_gather(table_rows, flat_index, chunk=3072):
    rows, width = table_rows.shape
    total = flat_index.shape[0]

    def kernel(index_ref, table_ref, out_ref, stage_ref):
        base = pl.program_id(0) * chunk

        def copy_rows(group, carry):
            first = pl.multiple_of(group * 8, 8)
            picked = [
                table_ref[pl.ds(index_ref[base + first + r], 1), :] for r in range(8)
            ]
            stage_ref[pl.ds(first, 8), :] = jnp.concatenate(picked, axis=0)
            return carry

        lax.fori_loop(0, chunk // 8, copy_rows, 0, unroll=8)
        for part in range(chunk // 128):
            out_ref[:, part * 128 : (part + 1) * 128] = stage_ref[
                part * 128 : (part + 1) * 128, :
            ].T

    return pl.pallas_call(
        kernel,
        out_shape=jax.ShapeDtypeStruct((width, total), table_rows.dtype),
        grid_spec=pltpu.PrefetchScalarGridSpec(
            num_scalar_prefetch=1,
            grid=(total // chunk,),
            in_specs=[pl.BlockSpec((rows, width), lambda i, index: (0, 0))],
            out_specs=pl.BlockSpec((width, chunk), lambda i, index: (0, i)),
            scratch_shapes=[pltpu.VMEM((chunk, width), table_rows.dtype)],
        ),
        cost_estimate=pl.CostEstimate(
            flops=0, transcendentals=0, bytes_accessed=4 * (rows * width + 2 * width * total)
        ),
    )(flat_index, table_rows)


def column_gather(table, index):
    rows, width = table.shape
    lanes = 128
    blocks = -(-width // lanes)
    padded_table = jnp.pad(table, ((0, 0), (0, blocks * lanes - width)))
    flat = index.reshape(-1)
    high = flat // lanes
    low = flat % lanes
    picks = (jnp.arange(lanes)[:, None] == low[None, :]).astype(jnp.float32)
    spread = jnp.dot(
        padded_table.reshape(rows * blocks, lanes), picks, precision=lax.Precision.HIGHEST
    ).reshape(rows, blocks, flat.shape[0])
    chosen = jnp.arange(blocks)[:, None] == high[None, :]
    gathered = jnp.sum(jnp.where(chosen[None], spread, 0.0), axis=1)
    return gathered.reshape((rows,) + index.shape)


def harmonics(vector):
    coord_x, coord_y, coord_z = (vector[0], vector[1], vector[2])
    radius_sq = coord_x * coord_x + coord_y * coord_y + coord_z * coord_z
    terms = [
        jnp.ones_like(coord_x),
        coord_x,
        coord_y,
        coord_z,
        ROOT_THREE * coord_x * coord_y,
        ROOT_THREE * coord_y * coord_z,
        0.5 * (3.0 * coord_z * coord_z - radius_sq),
        ROOT_THREE * coord_x * coord_z,
        0.5 * ROOT_THREE * (coord_x * coord_x - coord_y * coord_y),
        0.79 * coord_y * (3.0 * coord_x * coord_x - coord_y * coord_y),
        3.87 * coord_x * coord_y * coord_z,
        0.61 * coord_y * (4.0 * coord_z * coord_z - coord_x * coord_x - coord_y * coord_y),
        0.5
        * coord_z
        * (2.0 * coord_z * coord_z - 3.0 * coord_x * coord_x - 3.0 * coord_y * coord_y),
        0.61 * coord_x * (4.0 * coord_z * coord_z - coord_x * coord_x - coord_y * coord_y),
        1.94 * coord_z * (coord_x * coord_x - coord_y * coord_y),
        0.79 * coord_x * (coord_x * coord_x - 3.0 * coord_y * coord_y),
    ]
    return jnp.stack(terms)


def radial(vector, orders):
    radius_sq = jnp.sum(vector * vector, axis=0)
    decay = jnp.exp(-radius_sq / SPREAD)
    argument = 2.0 * decay - 1.0
    polys = [jnp.ones_like(argument), argument]
    for order_id in range(2, orders):
        polys.append(2.0 * argument * polys[-1] - polys[-2])
    return decay * jnp.stack(polys[:orders])


def pair_energy(vector, weights):
    basis = radial(vector, weights.shape[0])
    mixed = jnp.sum(weights * basis[:, None], axis=0)
    return jnp.sum(mixed * harmonics(vector), axis=0)


def atom_basis(separation, pair_mask, radial_weight):
    basis = radial(separation, radial_weight.shape[1])
    shaped = jnp.sum(radial_weight[:, :, None, None] * basis[None], axis=1) * pair_mask
    return jnp.sum(shaped[:, None] * harmonics(separation)[None], axis=2)


def adjoints(basis_sum, linear_weight, pair_coupling):
    per_harmonic = jnp.concatenate(
        [
            jnp.repeat(pair_coupling[degree_id : degree_id + 1], copies, axis=0)
            for degree_id, copies in enumerate((1, 3, 5, 7))
        ],
        axis=0,
    )
    by_harmonic = jnp.transpose(basis_sum, (1, 0, 2))
    forward = jnp.sum(
        jnp.transpose(per_harmonic, (1, 0, 2))[:, :, :, None] * by_harmonic[None], axis=2
    )
    backward = jnp.sum(
        jnp.transpose(per_harmonic, (2, 0, 1))[:, :, :, None] * by_harmonic[None], axis=2
    )
    energy = jnp.dot(linear_weight, basis_sum[:, 0, :], precision=lax.Precision.HIGHEST) + jnp.sum(
        basis_sum * forward, axis=(0, 1)
    )
    isotropic = (jnp.arange(basis_sum.shape[1]) == 0).astype(jnp.float32)
    adjoint = forward + backward + linear_weight[:, None, None] * isotropic[None, :, None]
    return (energy, adjoint)


def pair_forces(separation, pair_mask, own_weights, other_weights):
    own_grad = jax.grad(lambda vector: jnp.sum(pair_energy(vector, own_weights)))(separation)
    other_grad = jax.grad(lambda vector: jnp.sum(pair_energy(vector, other_weights)))(-separation)
    pieces = (own_grad - other_grad) * pair_mask
    return (
        jnp.sum(pieces, axis=1),
        jnp.einsum("aki,bki->ab", separation, pieces, precision=lax.Precision.HIGHEST),
    )


def substep(temp_ext, kappa_ext, heat_here, lattice_here, occupancy_here, lower_open, upper_open):
    centre = temp_ext[1:-1, 1:-1, 1:-1]
    centre_kappa = kappa_ext[1:-1, 1:-1, 1:-1]

    def face(beside_temp, beside_kappa):
        return 0.5 * (centre_kappa + beside_kappa) * (beside_temp - centre)

    divergence = (
        face(temp_ext[1:-1, 1:-1, 2:], kappa_ext[1:-1, 1:-1, 2:])
        + face(temp_ext[1:-1, 1:-1, :-2], kappa_ext[1:-1, 1:-1, :-2])
        + face(temp_ext[1:-1, 2:, 1:-1], kappa_ext[1:-1, 2:, 1:-1])
        + face(temp_ext[1:-1, :-2, 1:-1], kappa_ext[1:-1, :-2, 1:-1])
        + face(temp_ext[2:, 1:-1, 1:-1], kappa_ext[2:, 1:-1, 1:-1]) * upper_open
        + face(temp_ext[:-2, 1:-1, 1:-1], kappa_ext[:-2, 1:-1, 1:-1]) * lower_open
    )
    return centre + HEAT_STEP / centre * (
        divergence + heat_here - COUPLE * occupancy_here * (centre - lattice_here)
    )


def local(
    positions,
    velocities,
    neighbour_index,
    neighbour_count,
    ghost_list,
    brick_count,
    atom_cell,
    radial_weight,
    linear_weight,
    pair_coupling,
    electron_temp,
    conductivity,
    heating,
):
    atom_slots = positions.shape[1]
    ghosts = ghost_list.shape[0]
    neigh_depth = neighbour_index.shape[0]
    orders = radial_weight.shape[1]
    live_count = brick_count[0]
    alive_mask = (jnp.arange(atom_slots) < live_count).astype(jnp.float32)
    slot_ids = jnp.arange(27)
    offsets = jnp.stack(
        [slot_ids // 9 - 1, slot_ids // 3 % 3 - 1, slot_ids % 3 - 1], axis=1
    ).astype(jnp.float32)
    ghost_sent = jnp.take(positions, ghost_list, axis=1).reshape(1, 1, 1, 3, ghosts)
    framed = padded(ghost_sent, (("gz", 2), (GX, 0), (GY, 1)), 1, ("gz",))
    shifted = framed.reshape(27, 3, ghosts) + offsets[:, :, None]
    pos_table = jnp.concatenate(
        [positions, jnp.transpose(shifted, (1, 0, 2)).reshape(3, 27 * ghosts)], axis=1
    )
    separation = column_gather(pos_table, neighbour_index) - positions[:, None, :]
    pair_mask = (jnp.arange(neigh_depth)[:, None] < neighbour_count[None, :]).astype(jnp.float32)
    basis_sum = atom_basis(separation, pair_mask, radial_weight)
    energy, adjoint = adjoints(basis_sum, linear_weight, pair_coupling)
    reduced = jnp.sum(radial_weight.T[:, :, None, None] * adjoint[None], axis=1)
    own_table = reduced.reshape(orders * 16, atom_slots)
    picked = jnp.take(own_table, ghost_list, axis=1).reshape(1, 1, 1, orders * 16, ghosts)
    framed_adjoint = padded(picked, (("gz", 2), (GX, 0), (GY, 1)), 1, ("gz",))
    remote = framed_adjoint.reshape(27, orders * 16, ghosts)
    table_rows = jnp.concatenate(
        [own_table.T, jnp.transpose(remote, (0, 2, 1)).reshape(27 * ghosts, orders * 16)], axis=0
    )
    other_weights = row_gather(table_rows, neighbour_index.reshape(-1)).reshape(
        orders, 16, neigh_depth, atom_slots
    )
    forces, virial = pair_forces(
        separation, pair_mask, own_table.reshape(orders, 16, 1, atom_slots), other_weights
    )
    kicked = velocities + KICK * forces
    grid_shape = electron_temp.shape
    cell_total = grid_shape[0] * grid_shape[1] * grid_shape[2]
    cell_picks = (jnp.arange(cell_total)[:, None] == atom_cell[None, :]).astype(jnp.float32)
    per_cell = jnp.dot(
        cell_picks,
        jnp.stack([alive_mask * jnp.sum(kicked * kicked, axis=0), alive_mask], axis=1),
        precision=lax.Precision.HIGHEST,
    )
    kinetic = per_cell[:, 0]
    filled = per_cell[:, 1]
    lattice = (kinetic / (3.0 * jnp.maximum(filled, 1.0))).reshape(grid_shape)
    occupancy = jnp.minimum(filled, 1.0).reshape(grid_shape)
    depth_index = lax.axis_index("gz")
    depth_total = grid_shape[0] * lax.axis_size("gz")
    stacked = jnp.stack([electron_temp, conductivity, heating, lattice, occupancy])
    margins = padded(stacked, (("gz", 1), (GX, 3), (GY, 2)), SUBSTEPS)
    electron = margins[0]
    cond_ext = margins[1]
    heat_ext = margins[2]
    lattice_ext = margins[3]
    occupancy_ext = margins[4]
    for substep_id in range(SUBSTEPS):
        margin = SUBSTEPS - substep_id - 1
        heat_ext = heat_ext[1:-1, 1:-1, 1:-1]
        lattice_ext = lattice_ext[1:-1, 1:-1, 1:-1]
        occupancy_ext = occupancy_ext[1:-1, 1:-1, 1:-1]
        global_z = depth_index * grid_shape[0] - margin + jnp.arange(heat_ext.shape[0])
        lower_open = (global_z != 0).astype(jnp.float32)[:, None, None]
        upper_open = (global_z != depth_total - 1).astype(jnp.float32)[:, None, None]
        lower_open, upper_open = (lower_open, upper_open)
        electron = substep(
            electron,
            cond_ext * electron,
            heat_ext,
            lattice_ext,
            occupancy_ext,
            lower_open,
            upper_open,
        )
        cond_ext = cond_ext[1:-1, 1:-1, 1:-1]
    exchange_rate = RELAX * (electron - lattice) / (electron + lattice)
    scaling = jnp.dot(
        exchange_rate.reshape(1, -1), cell_picks, precision=lax.Precision.HIGHEST
    ).reshape(-1)
    new_velocity = kicked * (1.0 + scaling) * alive_mask
    packed = jnp.concatenate(
        [
            jnp.reshape(jnp.sum(energy * alive_mask), (1,)),
            virial.reshape(9),
            jnp.reshape(live_count.astype(jnp.float32), (1,)),
        ]
    )
    summed = by_axis(packed, GX_GY_GZ)
    totals = summed[:10] / summed[10]
    return (forces, new_velocity, electron, totals)


def solution(mesh):
    torus = Mesh(
        mesh.devices.reshape(2, 4, 8, 2, mesh.shape["gz"]), ("gx_0", "gx_1", "gy_0", "gy_1", "gz")
    )
    placed = (
        P(None, GX_GY_GZ),
        P(None, GX_GY_GZ),
        P(None, GX_GY_GZ),
        P(GX_GY_GZ),
        P(GX_GY_GZ),
        P(GX_GY_GZ),
        P(GX_GY_GZ),
        P(),
        P(),
        P(),
        P("gz", GY, GX),
        P("gz", GY, GX),
        P("gz", GY, GX),
    )
    return jax.shard_map(
        local,
        mesh=torus,
        in_specs=placed,
        out_specs=(P(None, GX_GY_GZ), P(None, GX_GY_GZ), P("gz", GY, GX), P()),
        check_vma=False,
    )
```

```python
import functools

import jax
import jax.numpy as jnp
from jax import lax
from jax.experimental import pallas as pl
from jax.experimental.pallas import tpu as pltpu
from jax.sharding import Mesh
from jax.sharding import PartitionSpec as P

SUBSTEPS = 4
GX_GY_GZ = ("gx_0", "gx_1", "gy_0", "gy_1", "gz")
GX = ("gx_0", "gx_1")
GY = ("gy_0", "gy_1")


HEAT_STEP = 0.15
COUPLE = 0.5
RELAX = 0.2
KICK = 0.05
SPREAD = 2.0
ROOT_THREE = 1.7320508


def padded(cells, sides, width, open_axes=()):
    for axis, dim in sides:
        count = lax.axis_size(axis)
        links = count if axis not in open_axes else count - 1
        head = lax.slice_in_dim(cells, 0, width, axis=dim)
        tail = lax.slice_in_dim(cells, cells.shape[dim] - width, cells.shape[dim], axis=dim)
        cells = jnp.concatenate(
            [
                lax.ppermute(tail, axis, [(i, (i + 1) % count) for i in range(links)]),
                cells,
                lax.ppermute(head, axis, [((i + 1) % count, i) for i in range(links)]),
            ],
            axis=dim,
        )
    return cells


def by_axis(shard, axes):
    return functools.reduce(lax.psum, axes, shard)


def group_sum(values, axes):
    count = lax.axis_size(axes)
    here = lax.axis_index(axes)
    received = [values] + [
        lax.ppermute(values, axes, [(j, (j - shift) % count) for j in range(count)])
        for shift in range(1, count)
    ]
    ordered = jnp.roll(jnp.stack(received), here, axis=0)
    return jnp.sum(ordered, axis=0)


def row_gather(table_rows, flat_index, chunk=3072):
    rows, width = table_rows.shape
    total = flat_index.shape[0]

    def kernel(index_ref, table_ref, out_ref, stage_ref):
        base = pl.program_id(0) * chunk

        def copy_rows(group, carry):
            first = pl.multiple_of(group * 8, 8)
            picked = [
                table_ref[pl.ds(index_ref[base + first + r], 1), :] for r in range(8)
            ]
            stage_ref[pl.ds(first, 8), :] = jnp.concatenate(picked, axis=0)
            return carry

        lax.fori_loop(0, chunk // 8, copy_rows, 0, unroll=8)
        for part in range(chunk // 128):
            out_ref[:, part * 128 : (part + 1) * 128] = stage_ref[
                part * 128 : (part + 1) * 128, :
            ].T

    return pl.pallas_call(
        kernel,
        out_shape=jax.ShapeDtypeStruct((width, total), table_rows.dtype),
        grid_spec=pltpu.PrefetchScalarGridSpec(
            num_scalar_prefetch=1,
            grid=(total // chunk,),
            in_specs=[pl.BlockSpec((rows, width), lambda i, index: (0, 0))],
            out_specs=pl.BlockSpec((width, chunk), lambda i, index: (0, i)),
            scratch_shapes=[pltpu.VMEM((chunk, width), table_rows.dtype)],
        ),
        cost_estimate=pl.CostEstimate(
            flops=0, transcendentals=0, bytes_accessed=4 * (rows * width + 2 * width * total)
        ),
    )(flat_index, table_rows)


def column_gather(table, index):
    rows, width = table.shape
    lanes = 128
    blocks = -(-width // lanes)
    padded_table = jnp.pad(table, ((0, 0), (0, blocks * lanes - width)))
    flat = index.reshape(-1)
    high = flat // lanes
    low = flat % lanes
    picks = (jnp.arange(lanes)[:, None] == low[None, :]).astype(jnp.float32)
    spread = jnp.dot(
        padded_table.reshape(rows * blocks, lanes), picks, precision=lax.Precision.HIGHEST
    ).reshape(rows, blocks, flat.shape[0])
    chosen = jnp.arange(blocks)[:, None] == high[None, :]
    gathered = jnp.sum(jnp.where(chosen[None], spread, 0.0), axis=1)
    return gathered.reshape((rows,) + index.shape)


def harmonics(vector):
    coord_x, coord_y, coord_z = (vector[0], vector[1], vector[2])
    radius_sq = coord_x * coord_x + coord_y * coord_y + coord_z * coord_z
    terms = [
        jnp.ones_like(coord_x),
        coord_x,
        coord_y,
        coord_z,
        ROOT_THREE * coord_x * coord_y,
        ROOT_THREE * coord_y * coord_z,
        0.5 * (3.0 * coord_z * coord_z - radius_sq),
        ROOT_THREE * coord_x * coord_z,
        0.5 * ROOT_THREE * (coord_x * coord_x - coord_y * coord_y),
        0.79 * coord_y * (3.0 * coord_x * coord_x - coord_y * coord_y),
        3.87 * coord_x * coord_y * coord_z,
        0.61 * coord_y * (4.0 * coord_z * coord_z - coord_x * coord_x - coord_y * coord_y),
        0.5
        * coord_z
        * (2.0 * coord_z * coord_z - 3.0 * coord_x * coord_x - 3.0 * coord_y * coord_y),
        0.61 * coord_x * (4.0 * coord_z * coord_z - coord_x * coord_x - coord_y * coord_y),
        1.94 * coord_z * (coord_x * coord_x - coord_y * coord_y),
        0.79 * coord_x * (coord_x * coord_x - 3.0 * coord_y * coord_y),
    ]
    return jnp.stack(terms)


def radial(vector, orders):
    radius_sq = jnp.sum(vector * vector, axis=0)
    decay = jnp.exp(-radius_sq / SPREAD)
    argument = 2.0 * decay - 1.0
    polys = [jnp.ones_like(argument), argument]
    for order_id in range(2, orders):
        polys.append(2.0 * argument * polys[-1] - polys[-2])
    return decay * jnp.stack(polys[:orders])


def pair_energy(vector, weights):
    basis = radial(vector, weights.shape[1])
    mixed = jnp.sum(weights * basis[None], axis=1)
    return jnp.sum(mixed * harmonics(vector), axis=0)


def atom_basis(separation, pair_mask, radial_weight):
    basis = radial(separation, radial_weight.shape[1])
    shaped = jnp.sum(radial_weight[:, :, None, None] * basis[None], axis=1) * pair_mask
    return jnp.sum(shaped[:, None] * harmonics(separation)[None], axis=2)


def adjoints(basis_sum, linear_weight, pair_coupling):
    per_harmonic = jnp.concatenate(
        [
            jnp.repeat(pair_coupling[degree_id : degree_id + 1], copies, axis=0)
            for degree_id, copies in enumerate((1, 3, 5, 7))
        ],
        axis=0,
    )
    by_harmonic = jnp.transpose(basis_sum, (1, 0, 2))
    forward = jnp.sum(
        jnp.transpose(per_harmonic, (1, 0, 2))[:, :, :, None] * by_harmonic[None], axis=2
    )
    backward = jnp.sum(
        jnp.transpose(per_harmonic, (2, 0, 1))[:, :, :, None] * by_harmonic[None], axis=2
    )
    energy = jnp.dot(linear_weight, basis_sum[:, 0, :], precision=lax.Precision.HIGHEST) + jnp.sum(
        basis_sum * forward, axis=(0, 1)
    )
    isotropic = (jnp.arange(basis_sum.shape[1]) == 0).astype(jnp.float32)
    adjoint = forward + backward + linear_weight[:, None, None] * isotropic[None, :, None]
    return (energy, adjoint)


def pair_forces(separation, pair_mask, own_weights, other_weights):
    own_grad = jax.grad(lambda vector: jnp.sum(pair_energy(vector, own_weights)))(separation)
    other_grad = jax.grad(lambda vector: jnp.sum(pair_energy(vector, other_weights)))(-separation)
    pieces = (own_grad - other_grad) * pair_mask
    return (
        jnp.sum(pieces, axis=1),
        jnp.einsum("aki,bki->ab", separation, pieces, precision=lax.Precision.HIGHEST),
    )


def substep(temp_ext, kappa_ext, heat_here, lattice_here, occupancy_here, lower_open, upper_open):
    centre = temp_ext[1:-1, 1:-1, 1:-1]
    centre_kappa = kappa_ext[1:-1, 1:-1, 1:-1]

    def face(beside_temp, beside_kappa):
        return 0.5 * (centre_kappa + beside_kappa) * (beside_temp - centre)

    divergence = (
        face(temp_ext[1:-1, 1:-1, 2:], kappa_ext[1:-1, 1:-1, 2:])
        + face(temp_ext[1:-1, 1:-1, :-2], kappa_ext[1:-1, 1:-1, :-2])
        + face(temp_ext[1:-1, 2:, 1:-1], kappa_ext[1:-1, 2:, 1:-1])
        + face(temp_ext[1:-1, :-2, 1:-1], kappa_ext[1:-1, :-2, 1:-1])
        + face(temp_ext[2:, 1:-1, 1:-1], kappa_ext[2:, 1:-1, 1:-1]) * upper_open
        + face(temp_ext[:-2, 1:-1, 1:-1], kappa_ext[:-2, 1:-1, 1:-1]) * lower_open
    )
    return centre + HEAT_STEP / centre * (
        divergence + heat_here - COUPLE * occupancy_here * (centre - lattice_here)
    )


def local(
    positions,
    velocities,
    neighbour_index,
    neighbour_count,
    ghost_list,
    brick_count,
    atom_cell,
    radial_weight,
    linear_weight,
    pair_coupling,
    electron_temp,
    conductivity,
    heating,
):
    atom_slots = positions.shape[1]
    ghosts = ghost_list.shape[0]
    neigh_depth = neighbour_index.shape[0]
    orders = radial_weight.shape[1]
    live_count = brick_count[0]
    alive_mask = (jnp.arange(atom_slots) < live_count).astype(jnp.float32)
    slot_ids = jnp.arange(27)
    offsets = jnp.stack(
        [slot_ids // 9 - 1, slot_ids // 3 % 3 - 1, slot_ids % 3 - 1], axis=1
    ).astype(jnp.float32)
    ghost_sent = jnp.take(positions, ghost_list, axis=1).reshape(1, 1, 1, 3, ghosts)
    framed = padded(ghost_sent, (("gz", 2), (GX, 0), (GY, 1)), 1, ("gz",))
    shifted = framed.reshape(27, 3, ghosts) + offsets[:, :, None]
    pos_table = jnp.concatenate(
        [positions, jnp.transpose(shifted, (1, 0, 2)).reshape(3, 27 * ghosts)], axis=1
    )
    separation = column_gather(pos_table, neighbour_index) - positions[:, None, :]
    pair_mask = (jnp.arange(neigh_depth)[:, None] < neighbour_count[None, :]).astype(jnp.float32)
    basis_sum = atom_basis(separation, pair_mask, radial_weight)
    energy, adjoint = adjoints(basis_sum, linear_weight, pair_coupling)
    reduced = jnp.sum(radial_weight.T[:, :, None, None] * adjoint[None], axis=1)
    own_table = jnp.transpose(reduced, (1, 0, 2)).reshape(16 * orders, atom_slots)
    picked = jnp.take(own_table, ghost_list, axis=1).reshape(1, 1, 1, orders * 16, ghosts)
    framed_adjoint = padded(picked, (("gz", 2), (GX, 0), (GY, 1)), 1, ("gz",))
    remote = framed_adjoint.reshape(27, orders * 16, ghosts)
    table_rows = jnp.concatenate(
        [own_table.T, jnp.transpose(remote, (0, 2, 1)).reshape(27 * ghosts, orders * 16)], axis=0
    )
    other_weights = row_gather(table_rows, neighbour_index.reshape(-1)).reshape(
        16, orders, neigh_depth, atom_slots
    )
    forces, virial = pair_forces(
        separation, pair_mask, own_table.reshape(16, orders, 1, atom_slots), other_weights
    )
    kicked = velocities + KICK * forces
    grid_shape = electron_temp.shape
    cell_total = grid_shape[0] * grid_shape[1] * grid_shape[2]
    cell_picks = (jnp.arange(cell_total)[:, None] == atom_cell[None, :]).astype(jnp.float32)
    per_cell = jnp.dot(
        cell_picks,
        jnp.stack([alive_mask * jnp.sum(kicked * kicked, axis=0), alive_mask], axis=1),
        precision=lax.Precision.HIGHEST,
    )
    kinetic = per_cell[:, 0]
    filled = per_cell[:, 1]
    lattice = (kinetic / (3.0 * jnp.maximum(filled, 1.0))).reshape(grid_shape)
    occupancy = jnp.minimum(filled, 1.0).reshape(grid_shape)
    depth_index = lax.axis_index("gz")
    depth_total = grid_shape[0] * lax.axis_size("gz")
    stacked = jnp.stack([electron_temp, conductivity, heating, lattice, occupancy])
    margins = padded(stacked, (("gz", 1), (GX, 3), (GY, 2)), SUBSTEPS)
    electron = margins[0]
    cond_ext = margins[1]
    heat_ext = margins[2]
    lattice_ext = margins[3]
    occupancy_ext = margins[4]
    for substep_id in range(SUBSTEPS):
        margin = SUBSTEPS - substep_id - 1
        heat_ext = heat_ext[1:-1, 1:-1, 1:-1]
        lattice_ext = lattice_ext[1:-1, 1:-1, 1:-1]
        occupancy_ext = occupancy_ext[1:-1, 1:-1, 1:-1]
        global_z = depth_index * grid_shape[0] - margin + jnp.arange(heat_ext.shape[0])
        lower_open = (global_z != 0).astype(jnp.float32)[:, None, None]
        upper_open = (global_z != depth_total - 1).astype(jnp.float32)[:, None, None]
        lower_open, upper_open = (lower_open, upper_open)
        electron = substep(
            electron,
            cond_ext * electron,
            heat_ext,
            lattice_ext,
            occupancy_ext,
            lower_open,
            upper_open,
        )
        cond_ext = cond_ext[1:-1, 1:-1, 1:-1]
    exchange_rate = RELAX * (electron - lattice) / (electron + lattice)
    scaling = jnp.dot(
        exchange_rate.reshape(1, -1), cell_picks, precision=lax.Precision.HIGHEST
    ).reshape(-1)
    new_velocity = kicked * (1.0 + scaling) * alive_mask
    packed = jnp.concatenate(
        [
            jnp.reshape(jnp.sum(energy * alive_mask), (1,)),
            virial.reshape(9),
            jnp.reshape(live_count.astype(jnp.float32), (1,)),
        ]
    )
    summed = by_axis(packed, GX_GY_GZ)
    totals = summed[:10] / summed[10]
    return (forces, new_velocity, electron, totals)


def solution(mesh):
    torus = Mesh(
        mesh.devices.reshape(2, 4, 8, 2, mesh.shape["gz"]), ("gx_0", "gx_1", "gy_0", "gy_1", "gz")
    )
    placed = (
        P(None, GX_GY_GZ),
        P(None, GX_GY_GZ),
        P(None, GX_GY_GZ),
        P(GX_GY_GZ),
        P(GX_GY_GZ),
        P(GX_GY_GZ),
        P(GX_GY_GZ),
        P(),
        P(),
        P(),
        P("gz", GY, GX),
        P("gz", GY, GX),
        P("gz", GY, GX),
    )
    return jax.shard_map(
        local,
        mesh=torus,
        in_specs=placed,
        out_specs=(P(None, GX_GY_GZ), P(None, GX_GY_GZ), P("gz", GY, GX), P()),
        check_vma=False,
    )
```

```python
import functools

import jax
import jax.numpy as jnp
from jax import lax
from jax.experimental import pallas as pl
from jax.experimental.pallas import tpu as pltpu
from jax.sharding import Mesh
from jax.sharding import PartitionSpec as P

SUBSTEPS = 4
GX_GY_GZ = ("gx_0", "gx_1", "gy_0", "gy_1", "gz")
GX = ("gx_0", "gx_1")
GY = ("gy_0", "gy_1")


HEAT_STEP = 0.15
COUPLE = 0.5
RELAX = 0.2
KICK = 0.05
SPREAD = 2.0
ROOT_THREE = 1.7320508


def padded(cells, sides, width, open_axes=()):
    for axis, dim in sides:
        count = lax.axis_size(axis)
        links = count if axis not in open_axes else count - 1
        head = lax.slice_in_dim(cells, 0, width, axis=dim)
        tail = lax.slice_in_dim(cells, cells.shape[dim] - width, cells.shape[dim], axis=dim)
        cells = jnp.concatenate(
            [
                lax.ppermute(tail, axis, [(i, (i + 1) % count) for i in range(links)]),
                cells,
                lax.ppermute(head, axis, [((i + 1) % count, i) for i in range(links)]),
            ],
            axis=dim,
        )
    return cells


def by_axis(shard, axes):
    return functools.reduce(lax.psum, axes, shard)


def group_sum(values, axes):
    count = lax.axis_size(axes)
    here = lax.axis_index(axes)
    received = [values] + [
        lax.ppermute(values, axes, [(j, (j - shift) % count) for j in range(count)])
        for shift in range(1, count)
    ]
    ordered = jnp.roll(jnp.stack(received), here, axis=0)
    return jnp.sum(ordered, axis=0)


def row_gather(table_rows, flat_index, chunk=4096):
    rows, width = table_rows.shape
    total = flat_index.shape[0]

    def kernel(index_ref, table_ref, out_ref, stage_ref):
        base = pl.program_id(0) * chunk

        def copy_rows(group, carry):
            first = pl.multiple_of(group * 8, 8)
            picked = [
                table_ref[pl.ds(index_ref[base + first + r], 1), :] for r in range(8)
            ]
            stage_ref[pl.ds(first, 8), :] = jnp.concatenate(picked, axis=0)
            return carry

        lax.fori_loop(0, chunk // 8, copy_rows, 0, unroll=16)
        for part in range(chunk // 128):
            out_ref[:, part * 128 : (part + 1) * 128] = stage_ref[
                part * 128 : (part + 1) * 128, :
            ].T

    return pl.pallas_call(
        kernel,
        out_shape=jax.ShapeDtypeStruct((width, total), table_rows.dtype),
        grid_spec=pltpu.PrefetchScalarGridSpec(
            num_scalar_prefetch=1,
            grid=(total // chunk,),
            in_specs=[pl.BlockSpec((rows, width), lambda i, index: (0, 0))],
            out_specs=pl.BlockSpec((width, chunk), lambda i, index: (0, i)),
            scratch_shapes=[pltpu.VMEM((chunk, width), table_rows.dtype)],
        ),
        cost_estimate=pl.CostEstimate(
            flops=0, transcendentals=0, bytes_accessed=4 * (rows * width + 2 * width * total)
        ),
    )(flat_index, table_rows)


def column_gather(table, index):
    rows, width = table.shape
    lanes = 128
    blocks = -(-width // lanes)
    padded_table = jnp.pad(table, ((0, 0), (0, blocks * lanes - width)))
    flat = index.reshape(-1)
    high = flat // lanes
    low = flat % lanes
    picks = (jnp.arange(lanes)[:, None] == low[None, :]).astype(jnp.float32)
    spread = jnp.dot(
        padded_table.reshape(rows * blocks, lanes), picks, precision=lax.Precision.HIGHEST
    ).reshape(rows, blocks, flat.shape[0])
    chosen = jnp.arange(blocks)[:, None] == high[None, :]
    gathered = jnp.sum(jnp.where(chosen[None], spread, 0.0), axis=1)
    return gathered.reshape((rows,) + index.shape)


def harmonics(vector):
    coord_x, coord_y, coord_z = (vector[0], vector[1], vector[2])
    radius_sq = coord_x * coord_x + coord_y * coord_y + coord_z * coord_z
    terms = [
        jnp.ones_like(coord_x),
        coord_x,
        coord_y,
        coord_z,
        ROOT_THREE * coord_x * coord_y,
        ROOT_THREE * coord_y * coord_z,
        0.5 * (3.0 * coord_z * coord_z - radius_sq),
        ROOT_THREE * coord_x * coord_z,
        0.5 * ROOT_THREE * (coord_x * coord_x - coord_y * coord_y),
        0.79 * coord_y * (3.0 * coord_x * coord_x - coord_y * coord_y),
        3.87 * coord_x * coord_y * coord_z,
        0.61 * coord_y * (4.0 * coord_z * coord_z - coord_x * coord_x - coord_y * coord_y),
        0.5
        * coord_z
        * (2.0 * coord_z * coord_z - 3.0 * coord_x * coord_x - 3.0 * coord_y * coord_y),
        0.61 * coord_x * (4.0 * coord_z * coord_z - coord_x * coord_x - coord_y * coord_y),
        1.94 * coord_z * (coord_x * coord_x - coord_y * coord_y),
        0.79 * coord_x * (coord_x * coord_x - 3.0 * coord_y * coord_y),
    ]
    return jnp.stack(terms)


def radial(vector, orders):
    radius_sq = jnp.sum(vector * vector, axis=0)
    decay = jnp.exp(-radius_sq / SPREAD)
    argument = 2.0 * decay - 1.0
    polys = [jnp.ones_like(argument), argument]
    for order_id in range(2, orders):
        polys.append(2.0 * argument * polys[-1] - polys[-2])
    return decay * jnp.stack(polys[:orders])


def pair_energy(vector, weights):
    basis = radial(vector, weights.shape[1])
    mixed = jnp.sum(weights * basis[None], axis=1)
    return jnp.sum(mixed * harmonics(vector), axis=0)


def atom_basis(separation, pair_mask, radial_weight):
    basis = radial(separation, radial_weight.shape[1])
    shaped = jnp.sum(radial_weight[:, :, None, None] * basis[None], axis=1) * pair_mask
    return jnp.sum(shaped[:, None] * harmonics(separation)[None], axis=2)


def adjoints(basis_sum, linear_weight, pair_coupling):
    per_harmonic = jnp.concatenate(
        [
            jnp.repeat(pair_coupling[degree_id : degree_id + 1], copies, axis=0)
            for degree_id, copies in enumerate((1, 3, 5, 7))
        ],
        axis=0,
    )
    by_harmonic = jnp.transpose(basis_sum, (1, 0, 2))
    forward = jnp.sum(
        jnp.transpose(per_harmonic, (1, 0, 2))[:, :, :, None] * by_harmonic[None], axis=2
    )
    backward = jnp.sum(
        jnp.transpose(per_harmonic, (2, 0, 1))[:, :, :, None] * by_harmonic[None], axis=2
    )
    energy = jnp.dot(linear_weight, basis_sum[:, 0, :], precision=lax.Precision.HIGHEST) + jnp.sum(
        basis_sum * forward, axis=(0, 1)
    )
    isotropic = (jnp.arange(basis_sum.shape[1]) == 0).astype(jnp.float32)
    adjoint = forward + backward + linear_weight[:, None, None] * isotropic[None, :, None]
    return (energy, adjoint)


def pair_forces(separation, pair_mask, own_weights, other_weights):
    own_grad = jax.grad(lambda vector: jnp.sum(pair_energy(vector, own_weights)))(separation)
    other_grad = jax.grad(lambda vector: jnp.sum(pair_energy(vector, other_weights)))(-separation)
    pieces = (own_grad - other_grad) * pair_mask
    return (
        jnp.sum(pieces, axis=1),
        jnp.einsum("aki,bki->ab", separation, pieces, precision=lax.Precision.HIGHEST),
    )


def substep(temp_ext, kappa_ext, heat_here, lattice_here, occupancy_here, lower_open, upper_open):
    centre = temp_ext[1:-1, 1:-1, 1:-1]
    centre_kappa = kappa_ext[1:-1, 1:-1, 1:-1]

    def face(beside_temp, beside_kappa):
        return 0.5 * (centre_kappa + beside_kappa) * (beside_temp - centre)

    divergence = (
        face(temp_ext[1:-1, 1:-1, 2:], kappa_ext[1:-1, 1:-1, 2:])
        + face(temp_ext[1:-1, 1:-1, :-2], kappa_ext[1:-1, 1:-1, :-2])
        + face(temp_ext[1:-1, 2:, 1:-1], kappa_ext[1:-1, 2:, 1:-1])
        + face(temp_ext[1:-1, :-2, 1:-1], kappa_ext[1:-1, :-2, 1:-1])
        + face(temp_ext[2:, 1:-1, 1:-1], kappa_ext[2:, 1:-1, 1:-1]) * upper_open
        + face(temp_ext[:-2, 1:-1, 1:-1], kappa_ext[:-2, 1:-1, 1:-1]) * lower_open
    )
    return centre + HEAT_STEP / centre * (
        divergence + heat_here - COUPLE * occupancy_here * (centre - lattice_here)
    )


def local(
    positions,
    velocities,
    neighbour_index,
    neighbour_count,
    ghost_list,
    brick_count,
    atom_cell,
    radial_weight,
    linear_weight,
    pair_coupling,
    electron_temp,
    conductivity,
    heating,
):
    atom_slots = positions.shape[1]
    ghosts = ghost_list.shape[0]
    neigh_depth = neighbour_index.shape[0]
    orders = radial_weight.shape[1]
    live_count = brick_count[0]
    alive_mask = (jnp.arange(atom_slots) < live_count).astype(jnp.float32)
    slot_ids = jnp.arange(27)
    offsets = jnp.stack(
        [slot_ids // 9 - 1, slot_ids // 3 % 3 - 1, slot_ids % 3 - 1], axis=1
    ).astype(jnp.float32)
    ghost_sent = jnp.take(positions, ghost_list, axis=1).reshape(1, 1, 1, 3, ghosts)
    framed = padded(ghost_sent, (("gz", 2), (GX, 0), (GY, 1)), 1, ("gz",))
    shifted = framed.reshape(27, 3, ghosts) + offsets[:, :, None]
    pos_table = jnp.concatenate(
        [positions, jnp.transpose(shifted, (1, 0, 2)).reshape(3, 27 * ghosts)], axis=1
    )
    separation = column_gather(pos_table, neighbour_index) - positions[:, None, :]
    pair_mask = (jnp.arange(neigh_depth)[:, None] < neighbour_count[None, :]).astype(jnp.float32)
    basis_sum = atom_basis(separation, pair_mask, radial_weight)
    energy, adjoint = adjoints(basis_sum, linear_weight, pair_coupling)
    reduced = jnp.sum(radial_weight.T[:, :, None, None] * adjoint[None], axis=1)
    own_table = jnp.transpose(reduced, (1, 0, 2)).reshape(16 * orders, atom_slots)
    picked = jnp.take(own_table, ghost_list, axis=1).reshape(1, 1, 1, orders * 16, ghosts)
    framed_adjoint = padded(picked, (("gz", 2), (GX, 0), (GY, 1)), 1, ("gz",))
    remote = framed_adjoint.reshape(27, orders * 16, ghosts)
    table_rows = jnp.concatenate(
        [own_table.T, jnp.transpose(remote, (0, 2, 1)).reshape(27 * ghosts, orders * 16)], axis=0
    )
    other_weights = row_gather(table_rows, neighbour_index.reshape(-1)).reshape(
        16, orders, neigh_depth, atom_slots
    )
    forces, virial = pair_forces(
        separation, pair_mask, own_table.reshape(16, orders, 1, atom_slots), other_weights
    )
    kicked = velocities + KICK * forces
    grid_shape = electron_temp.shape
    cell_total = grid_shape[0] * grid_shape[1] * grid_shape[2]
    cell_picks = (jnp.arange(cell_total)[:, None] == atom_cell[None, :]).astype(jnp.float32)
    per_cell = jnp.dot(
        cell_picks,
        jnp.stack([alive_mask * jnp.sum(kicked * kicked, axis=0), alive_mask], axis=1),
        precision=lax.Precision.HIGHEST,
    )
    kinetic = per_cell[:, 0]
    filled = per_cell[:, 1]
    lattice = (kinetic / (3.0 * jnp.maximum(filled, 1.0))).reshape(grid_shape)
    occupancy = jnp.minimum(filled, 1.0).reshape(grid_shape)
    depth_index = lax.axis_index("gz")
    depth_total = grid_shape[0] * lax.axis_size("gz")
    stacked = jnp.stack([electron_temp, conductivity, heating, lattice, occupancy])
    margins = padded(stacked, (("gz", 1), (GX, 3), (GY, 2)), SUBSTEPS)
    electron = margins[0]
    cond_ext = margins[1]
    heat_ext = margins[2]
    lattice_ext = margins[3]
    occupancy_ext = margins[4]
    for substep_id in range(SUBSTEPS):
        margin = SUBSTEPS - substep_id - 1
        heat_ext = heat_ext[1:-1, 1:-1, 1:-1]
        lattice_ext = lattice_ext[1:-1, 1:-1, 1:-1]
        occupancy_ext = occupancy_ext[1:-1, 1:-1, 1:-1]
        global_z = depth_index * grid_shape[0] - margin + jnp.arange(heat_ext.shape[0])
        lower_open = (global_z != 0).astype(jnp.float32)[:, None, None]
        upper_open = (global_z != depth_total - 1).astype(jnp.float32)[:, None, None]
        lower_open, upper_open = (lower_open, upper_open)
        electron = substep(
            electron,
            cond_ext * electron,
            heat_ext,
            lattice_ext,
            occupancy_ext,
            lower_open,
            upper_open,
        )
        cond_ext = cond_ext[1:-1, 1:-1, 1:-1]
    exchange_rate = RELAX * (electron - lattice) / (electron + lattice)
    scaling = jnp.dot(
        exchange_rate.reshape(1, -1), cell_picks, precision=lax.Precision.HIGHEST
    ).reshape(-1)
    new_velocity = kicked * (1.0 + scaling) * alive_mask
    packed = jnp.concatenate(
        [
            jnp.reshape(jnp.sum(energy * alive_mask), (1,)),
            virial.reshape(9),
            jnp.reshape(live_count.astype(jnp.float32), (1,)),
        ]
    )
    summed = by_axis(packed, GX_GY_GZ)
    totals = summed[:10] / summed[10]
    return (forces, new_velocity, electron, totals)


def solution(mesh):
    torus = Mesh(
        mesh.devices.reshape(2, 4, 8, 2, mesh.shape["gz"]), ("gx_0", "gx_1", "gy_0", "gy_1", "gz")
    )
    placed = (
        P(None, GX_GY_GZ),
        P(None, GX_GY_GZ),
        P(None, GX_GY_GZ),
        P(GX_GY_GZ),
        P(GX_GY_GZ),
        P(GX_GY_GZ),
        P(GX_GY_GZ),
        P(),
        P(),
        P(),
        P("gz", GY, GX),
        P("gz", GY, GX),
        P("gz", GY, GX),
    )
    return jax.shard_map(
        local,
        mesh=torus,
        in_specs=placed,
        out_specs=(P(None, GX_GY_GZ), P(None, GX_GY_GZ), P("gz", GY, GX), P()),
        check_vma=False,
    )
```

```python
import functools

import jax
import jax.numpy as jnp
from jax import lax
from jax.experimental import pallas as pl
from jax.experimental.pallas import tpu as pltpu
from jax.sharding import Mesh
from jax.sharding import PartitionSpec as P

SUBSTEPS = 4
GX_GY_GZ = ("gx_0", "gx_1", "gy_0", "gy_1", "gz")
GX = ("gx_0", "gx_1")
GY = ("gy_0", "gy_1")


HEAT_STEP = 0.15
COUPLE = 0.5
RELAX = 0.2
KICK = 0.05
SPREAD = 2.0
ROOT_THREE = 1.7320508


def padded(cells, sides, width, open_axes=()):
    for axis, dim in sides:
        count = lax.axis_size(axis)
        links = count if axis not in open_axes else count - 1
        head = lax.slice_in_dim(cells, 0, width, axis=dim)
        tail = lax.slice_in_dim(cells, cells.shape[dim] - width, cells.shape[dim], axis=dim)
        cells = jnp.concatenate(
            [
                lax.ppermute(tail, axis, [(i, (i + 1) % count) for i in range(links)]),
                cells,
                lax.ppermute(head, axis, [((i + 1) % count, i) for i in range(links)]),
            ],
            axis=dim,
        )
    return cells


def by_axis(shard, axes):
    return functools.reduce(lax.psum, axes, shard)


def group_sum(values, axes):
    count = lax.axis_size(axes)
    here = lax.axis_index(axes)
    received = [values] + [
        lax.ppermute(values, axes, [(j, (j - shift) % count) for j in range(count)])
        for shift in range(1, count)
    ]
    ordered = jnp.roll(jnp.stack(received), here, axis=0)
    return jnp.sum(ordered, axis=0)


def row_gather(table_rows, flat_index, chunk=3072):
    rows, width = table_rows.shape
    total = flat_index.shape[0]

    def kernel(index_ref, table_ref, out_ref, stage_ref):
        base = pl.program_id(0) * chunk

        def copy_rows(group, carry):
            first = pl.multiple_of(group * 8, 8)
            picked = [
                table_ref[pl.ds(index_ref[base + first + r], 1), :] for r in range(8)
            ]
            stage_ref[pl.ds(first, 8), :] = jnp.concatenate(picked, axis=0)
            return carry

        lax.fori_loop(0, chunk // 8, copy_rows, 0, unroll=8)
        for part in range(chunk // 128):
            out_ref[:, part * 128 : (part + 1) * 128] = stage_ref[
                part * 128 : (part + 1) * 128, :
            ].T

    return pl.pallas_call(
        kernel,
        out_shape=jax.ShapeDtypeStruct((width, total), table_rows.dtype),
        grid_spec=pltpu.PrefetchScalarGridSpec(
            num_scalar_prefetch=1,
            grid=(total // chunk,),
            in_specs=[pl.BlockSpec((rows, width), lambda i, index: (0, 0))],
            out_specs=pl.BlockSpec((width, chunk), lambda i, index: (0, i)),
            scratch_shapes=[pltpu.VMEM((chunk, width), table_rows.dtype)],
        ),
        cost_estimate=pl.CostEstimate(
            flops=0, transcendentals=0, bytes_accessed=4 * (rows * width + 2 * width * total)
        ),
    )(flat_index, table_rows)


def column_gather(table, index):
    rows, width = table.shape
    lanes = 128
    blocks = -(-width // lanes)
    padded_table = jnp.pad(table, ((0, 0), (0, blocks * lanes - width)))
    flat = index.reshape(-1)
    high = flat // lanes
    low = flat % lanes
    picks = (jnp.arange(lanes)[:, None] == low[None, :]).astype(jnp.float32)
    spread = jnp.dot(
        padded_table.reshape(rows * blocks, lanes), picks, precision=lax.Precision.HIGHEST
    ).reshape(rows, blocks, flat.shape[0])
    chosen = jnp.arange(blocks)[:, None] == high[None, :]
    gathered = jnp.sum(jnp.where(chosen[None], spread, 0.0), axis=1)
    return gathered.reshape((rows,) + index.shape)


def harmonics(vector):
    coord_x, coord_y, coord_z = (vector[0], vector[1], vector[2])
    radius_sq = coord_x * coord_x + coord_y * coord_y + coord_z * coord_z
    terms = [
        jnp.ones_like(coord_x),
        coord_x,
        coord_y,
        coord_z,
        ROOT_THREE * coord_x * coord_y,
        ROOT_THREE * coord_y * coord_z,
        0.5 * (3.0 * coord_z * coord_z - radius_sq),
        ROOT_THREE * coord_x * coord_z,
        0.5 * ROOT_THREE * (coord_x * coord_x - coord_y * coord_y),
        0.79 * coord_y * (3.0 * coord_x * coord_x - coord_y * coord_y),
        3.87 * coord_x * coord_y * coord_z,
        0.61 * coord_y * (4.0 * coord_z * coord_z - coord_x * coord_x - coord_y * coord_y),
        0.5
        * coord_z
        * (2.0 * coord_z * coord_z - 3.0 * coord_x * coord_x - 3.0 * coord_y * coord_y),
        0.61 * coord_x * (4.0 * coord_z * coord_z - coord_x * coord_x - coord_y * coord_y),
        1.94 * coord_z * (coord_x * coord_x - coord_y * coord_y),
        0.79 * coord_x * (coord_x * coord_x - 3.0 * coord_y * coord_y),
    ]
    return jnp.stack(terms)


def radial(vector, orders):
    radius_sq = jnp.sum(vector * vector, axis=0)
    decay = jnp.exp(-radius_sq / SPREAD)
    argument = 2.0 * decay - 1.0
    polys = [jnp.ones_like(argument), argument]
    for order_id in range(2, orders):
        polys.append(2.0 * argument * polys[-1] - polys[-2])
    return decay * jnp.stack(polys[:orders])


def pair_energy(vector, weights):
    basis = radial(vector, weights.shape[1])
    mixed = jnp.sum(weights * basis[None], axis=1)
    return jnp.sum(mixed * harmonics(vector), axis=0)


def atom_basis(separation, pair_mask, radial_weight):
    basis = radial(separation, radial_weight.shape[1])
    shaped = jnp.sum(radial_weight[:, :, None, None] * basis[None], axis=1) * pair_mask
    return jnp.sum(shaped[:, None] * harmonics(separation)[None], axis=2)


def adjoints(basis_sum, linear_weight, pair_coupling):
    per_harmonic = jnp.concatenate(
        [
            jnp.repeat(pair_coupling[degree_id : degree_id + 1], copies, axis=0)
            for degree_id, copies in enumerate((1, 3, 5, 7))
        ],
        axis=0,
    )
    by_harmonic = jnp.transpose(basis_sum, (1, 0, 2))
    forward = jnp.sum(
        jnp.transpose(per_harmonic, (1, 0, 2))[:, :, :, None] * by_harmonic[None], axis=2
    )
    backward = jnp.sum(
        jnp.transpose(per_harmonic, (2, 0, 1))[:, :, :, None] * by_harmonic[None], axis=2
    )
    energy = jnp.dot(linear_weight, basis_sum[:, 0, :], precision=lax.Precision.HIGHEST) + jnp.sum(
        basis_sum * forward, axis=(0, 1)
    )
    isotropic = (jnp.arange(basis_sum.shape[1]) == 0).astype(jnp.float32)
    adjoint = forward + backward + linear_weight[:, None, None] * isotropic[None, :, None]
    return (energy, adjoint)


def pair_forces(separation, pair_mask, own_weights, other_weights):
    own_grad = jax.grad(lambda vector: jnp.sum(pair_energy(vector, own_weights)))(separation)
    own_pieces = own_grad * pair_mask
    own_force = jnp.sum(own_pieces, axis=1)
    own_virial = jnp.einsum(
        "aki,bki->ab", separation, own_pieces, precision=lax.Precision.HIGHEST
    )
    other_grad = jax.grad(lambda vector: jnp.sum(pair_energy(vector, other_weights)))(-separation)
    other_pieces = other_grad * pair_mask
    return (
        own_force - jnp.sum(other_pieces, axis=1),
        own_virial
        - jnp.einsum("aki,bki->ab", separation, other_pieces, precision=lax.Precision.HIGHEST),
    )


def substep(temp_ext, kappa_ext, heat_here, lattice_here, occupancy_here, lower_open, upper_open):
    centre = temp_ext[1:-1, 1:-1, 1:-1]
    centre_kappa = kappa_ext[1:-1, 1:-1, 1:-1]

    def face(beside_temp, beside_kappa):
        return 0.5 * (centre_kappa + beside_kappa) * (beside_temp - centre)

    divergence = (
        face(temp_ext[1:-1, 1:-1, 2:], kappa_ext[1:-1, 1:-1, 2:])
        + face(temp_ext[1:-1, 1:-1, :-2], kappa_ext[1:-1, 1:-1, :-2])
        + face(temp_ext[1:-1, 2:, 1:-1], kappa_ext[1:-1, 2:, 1:-1])
        + face(temp_ext[1:-1, :-2, 1:-1], kappa_ext[1:-1, :-2, 1:-1])
        + face(temp_ext[2:, 1:-1, 1:-1], kappa_ext[2:, 1:-1, 1:-1]) * upper_open
        + face(temp_ext[:-2, 1:-1, 1:-1], kappa_ext[:-2, 1:-1, 1:-1]) * lower_open
    )
    return centre + HEAT_STEP / centre * (
        divergence + heat_here - COUPLE * occupancy_here * (centre - lattice_here)
    )


def local(
    positions,
    velocities,
    neighbour_index,
    neighbour_count,
    ghost_list,
    brick_count,
    atom_cell,
    radial_weight,
    linear_weight,
    pair_coupling,
    electron_temp,
    conductivity,
    heating,
):
    atom_slots = positions.shape[1]
    ghosts = ghost_list.shape[0]
    neigh_depth = neighbour_index.shape[0]
    orders = radial_weight.shape[1]
    live_count = brick_count[0]
    alive_mask = (jnp.arange(atom_slots) < live_count).astype(jnp.float32)
    slot_ids = jnp.arange(27)
    offsets = jnp.stack(
        [slot_ids // 9 - 1, slot_ids // 3 % 3 - 1, slot_ids % 3 - 1], axis=1
    ).astype(jnp.float32)
    ghost_sent = jnp.take(positions, ghost_list, axis=1).reshape(1, 1, 1, 3, ghosts)
    framed = padded(ghost_sent, (("gz", 2), (GX, 0), (GY, 1)), 1, ("gz",))
    shifted = framed.reshape(27, 3, ghosts) + offsets[:, :, None]
    pos_table = jnp.concatenate(
        [positions, jnp.transpose(shifted, (1, 0, 2)).reshape(3, 27 * ghosts)], axis=1
    )
    separation = column_gather(pos_table, neighbour_index) - positions[:, None, :]
    pair_mask = (jnp.arange(neigh_depth)[:, None] < neighbour_count[None, :]).astype(jnp.float32)
    basis_sum = atom_basis(separation, pair_mask, radial_weight)
    energy, adjoint = adjoints(basis_sum, linear_weight, pair_coupling)
    reduced = jnp.sum(radial_weight.T[:, :, None, None] * adjoint[None], axis=1)
    own_table = jnp.transpose(reduced, (1, 0, 2)).reshape(16 * orders, atom_slots)
    picked = jnp.take(own_table, ghost_list, axis=1).reshape(1, 1, 1, orders * 16, ghosts)
    framed_adjoint = padded(picked, (("gz", 2), (GX, 0), (GY, 1)), 1, ("gz",))
    remote = framed_adjoint.reshape(27, orders * 16, ghosts)
    table_rows = jnp.concatenate(
        [own_table.T, jnp.transpose(remote, (0, 2, 1)).reshape(27 * ghosts, orders * 16)], axis=0
    )
    other_weights = row_gather(table_rows, neighbour_index.reshape(-1)).reshape(
        16, orders, neigh_depth, atom_slots
    )
    forces, virial = pair_forces(
        separation, pair_mask, own_table.reshape(16, orders, 1, atom_slots), other_weights
    )
    kicked = velocities + KICK * forces
    grid_shape = electron_temp.shape
    cell_total = grid_shape[0] * grid_shape[1] * grid_shape[2]
    cell_picks = (jnp.arange(cell_total)[:, None] == atom_cell[None, :]).astype(jnp.float32)
    per_cell = jnp.dot(
        cell_picks,
        jnp.stack([alive_mask * jnp.sum(kicked * kicked, axis=0), alive_mask], axis=1),
        precision=lax.Precision.HIGHEST,
    )
    kinetic = per_cell[:, 0]
    filled = per_cell[:, 1]
    lattice = (kinetic / (3.0 * jnp.maximum(filled, 1.0))).reshape(grid_shape)
    occupancy = jnp.minimum(filled, 1.0).reshape(grid_shape)
    depth_index = lax.axis_index("gz")
    depth_total = grid_shape[0] * lax.axis_size("gz")
    stacked = jnp.stack([electron_temp, conductivity, heating, lattice, occupancy])
    margins = padded(stacked, (("gz", 1), (GX, 3), (GY, 2)), SUBSTEPS)
    electron = margins[0]
    cond_ext = margins[1]
    heat_ext = margins[2]
    lattice_ext = margins[3]
    occupancy_ext = margins[4]
    for substep_id in range(SUBSTEPS):
        margin = SUBSTEPS - substep_id - 1
        heat_ext = heat_ext[1:-1, 1:-1, 1:-1]
        lattice_ext = lattice_ext[1:-1, 1:-1, 1:-1]
        occupancy_ext = occupancy_ext[1:-1, 1:-1, 1:-1]
        global_z = depth_index * grid_shape[0] - margin + jnp.arange(heat_ext.shape[0])
        lower_open = (global_z != 0).astype(jnp.float32)[:, None, None]
        upper_open = (global_z != depth_total - 1).astype(jnp.float32)[:, None, None]
        lower_open, upper_open = (lower_open, upper_open)
        electron = substep(
            electron,
            cond_ext * electron,
            heat_ext,
            lattice_ext,
            occupancy_ext,
            lower_open,
            upper_open,
        )
        cond_ext = cond_ext[1:-1, 1:-1, 1:-1]
    exchange_rate = RELAX * (electron - lattice) / (electron + lattice)
    scaling = jnp.dot(
        exchange_rate.reshape(1, -1), cell_picks, precision=lax.Precision.HIGHEST
    ).reshape(-1)
    new_velocity = kicked * (1.0 + scaling) * alive_mask
    packed = jnp.concatenate(
        [
            jnp.reshape(jnp.sum(energy * alive_mask), (1,)),
            virial.reshape(9),
            jnp.reshape(live_count.astype(jnp.float32), (1,)),
        ]
    )
    summed = by_axis(packed, GX_GY_GZ)
    totals = summed[:10] / summed[10]
    return (forces, new_velocity, electron, totals)


def solution(mesh):
    torus = Mesh(
        mesh.devices.reshape(2, 4, 8, 2, mesh.shape["gz"]), ("gx_0", "gx_1", "gy_0", "gy_1", "gz")
    )
    placed = (
        P(None, GX_GY_GZ),
        P(None, GX_GY_GZ),
        P(None, GX_GY_GZ),
        P(GX_GY_GZ),
        P(GX_GY_GZ),
        P(GX_GY_GZ),
        P(GX_GY_GZ),
        P(),
        P(),
        P(),
        P("gz", GY, GX),
        P("gz", GY, GX),
        P("gz", GY, GX),
    )
    return jax.shard_map(
        local,
        mesh=torus,
        in_specs=placed,
        out_specs=(P(None, GX_GY_GZ), P(None, GX_GY_GZ), P("gz", GY, GX), P()),
        check_vma=False,
    )
```
